512 devices in a mesh: chan: 128 (over x, z_hi, y), win: 4 (over z_lo, core).
Axes of the slice: x: 4, y: 8, z: 8 (z_hi: 4, z_lo: 2; z = z_hi * 2 + z_lo), core: 2. Of those that a mesh axis runs over, the one named last changes fastest.
Arguments:
- strain: bfloat16 [6144, 4, 1024], P('chan', 'win'), may hold values from -384 to 384
- seg_ids: int32 [6144], replicated, may hold values from 0 to 511, never falling along the last dimension, each value on 1 to 24 neighbouring positions
- dead: int32 [512], replicated, may hold values 0 or 1
- radius: int32 [6144], P('chan'), may hold values from 1 to 8, as said below
Outputs:
- cross_spectra: bfloat16 [4, 2, 6144, 6144], P('win', None, 'chan')
The draws below stay inside these ranges and needn't reach their ends.
Inputs may be any that keep to these rules, and one draw needn't show every extreme that they name: `seg_ids`: segment numbers never fall along the fiber; a change of segment between neighbouring channels marks a splice. Every segment has 1 to 24 channels, and one has exactly that many. Some channel has radius 8.
All inputs are finite; a program needn't handle non-finite values.
Results may differ from the reference program's by a relative error of at most 0.0023.
Values may be sent and summed in bfloat16 or wider, within the bound.
No kernel may reach another device: no remote copies, remote signals or barrier semaphores. Data moves between devices by JAX's collectives and lax.ppermute only.
A program may use at most 64 MiB of HBM per device.

```python
import math
import jax
import jax.numpy as jnp
import numpy as np
from jax import lax

CHAN_DEV = 48
SAMPLES = 1024
FREQ_BINS = 128
FIRST_BIN = 8
SMOOTH_BINS = 4
MOST_REACH = 8
SEG_DEV = 4
CHANNELS = 6144
WINDOWS = 4
SEGMENTS = 512
BANDS = 4
BAND_BINS = 32


def draw_strain(key, part):
    keys = jax.random.split(key, 3)
    chan_scale = jnp.exp(jax.random.uniform(keys[0], (CHANNELS, 1, 1), minval=math.log(0.25), maxval=math.log(2.5)))
    window_scale = jnp.exp(jax.random.uniform(keys[1], (CHANNELS, WINDOWS, 1), minval=math.log(0.5), maxval=math.log(2.0)))
    noise = jax.random.truncated_normal(keys[2], -5.0, 5.0, (CHANNELS, WINDOWS, SAMPLES))
    sample_pos = jnp.arange(SAMPLES).astype(jnp.float32)
    edge_taper = 0.5 - 0.5 * jnp.cos(2.0 * math.pi / SAMPLES * (sample_pos + 0.5))
    envelope = 1.0 / jnp.maximum(edge_taper, 1.0 / 16.0)
    values = chan_scale * window_scale * noise * envelope[None, None, :]
    return jnp.clip(values, -384.0, 384.0).astype(jnp.bfloat16)


def draw_radius(key, part):
    spans = jax.random.randint(key, (CHANNELS,), 1, MOST_REACH + 1)
    chosen = jax.random.randint(jax.random.fold_in(key, 7), (), 0, CHANNELS)
    return jnp.where(jnp.arange(CHANNELS) == chosen, MOST_REACH, spans).astype(jnp.int32)


def touch_ends(drawn, rng, smallest, top_value):
    extent = drawn.shape
    index_at = [jax.random.randint(jax.random.fold_in(rng, axis), (), 0, extent[axis]) for axis in range(len(extent))]
    drawn = drawn.at[tuple(index_at)].set(smallest)
    longest = extent.index(max(extent))
    index_at[longest] = (index_at[longest] + 1) % extent[longest]
    return drawn.at[tuple(index_at)].set(top_value)


def length_profile(count, total, bound, skew):
    portions = [(1 << 20) // math.isqrt(grade ** skew) + 1 for grade in range(2, count + 1)]
    spare, given = total - bound - (count - 1), [1] * (count - 1)
    while spare > 0:
        movable = [i for i in range(count - 1) if given[i] < bound]
        pool, budget = sum([portions[i] for i in movable]), spare
        for i in movable:
            extra = min(bound - given[i], max(1, budget * portions[i] // pool), spare)
            given[i] = given[i] + extra
            spare = spare - extra
    return np.array([bound] + given)


def uneven_parts(key, amount, total, most, lean):
    if amount == 2:
        one = jax.random.randint(key, (), max(1, total - most), min(most, total - 1) + 1)
        return jnp.stack([one, total - one])
    sizes = jnp.asarray(length_profile(amount, total, most, lean), jnp.int32)
    twos = (amount - 1) // 2
    source_of, taker = sizes[1:1 + 2 * twos:2], sizes[2:2 + 2 * twos:2]
    margin = jnp.minimum(source_of - 1, most - taker)
    shifted = jax.random.randint(jax.random.fold_in(key, 1), (twos,), 0, 1 << 20) % (margin + 1)
    sizes = sizes.at[1:1 + 2 * twos:2].set(source_of - shifted).at[2:2 + 2 * twos:2].set(taker + shifted)
    return sizes[jax.random.permutation(jax.random.fold_in(key, 2), amount)]


def setup_inputs(seed: int = 0) -> dict:
    streams_of = jax.random.split(jax.random.key(seed), 5)
    return {
        "strain": draw_strain(jax.random.fold_in(streams_of[4], 71), 0),
        "seg_ids": jnp.searchsorted(jnp.cumsum(uneven_parts(streams_of[1], SEGMENTS, CHANNELS, 2 * CHAN_DEV // SEG_DEV, 0)), jnp.arange(CHANNELS), side="right").astype(jnp.int32),
        "dead": touch_ends((jax.random.randint(streams_of[2], (SEGMENTS,), 0, 8) < 1).astype(jnp.int32), jax.random.fold_in(streams_of[2], 1), 0, 1),
        "radius": draw_radius(jax.random.fold_in(streams_of[4], 71), 0),
    }


FLOOR_POWER = 0.01

def fourier_table():
    sample_ids = jnp.arange(SAMPLES, dtype=jnp.int32)
    bin_ids = FIRST_BIN + jnp.arange(FREQ_BINS, dtype=jnp.int32)
    phase_ids = sample_ids[:, None] * bin_ids[None, :] % SAMPLES
    angles = 2.0 * jnp.pi / SAMPLES * phase_ids.astype(jnp.float32)
    taper = 0.5 - 0.5 * jnp.cos(2.0 * jnp.pi / SAMPLES * (sample_ids.astype(jnp.float32) + 0.5))
    weights = taper[:, None] / jnp.sqrt(jnp.float32(SAMPLES))
    return jnp.concatenate([weights * jnp.cos(angles), -weights * jnp.sin(angles)], axis=1)

def smoothing_table():
    bin_ids = jnp.arange(FREQ_BINS, dtype=jnp.int32)
    nearby = (jnp.abs(bin_ids[:, None] - bin_ids[None, :]) <= SMOOTH_BINS).astype(jnp.float32)
    return nearby / lax.optimization_barrier(jnp.sum(nearby, axis=0, keepdims=True))

def swapped_parts(flat, windows):
    parts = flat.reshape(flat.shape[:-1] + (windows, 2, -1))
    turned = jnp.stack([-parts[..., 1, :], parts[..., 0, :]], axis=-2)
    return turned.reshape(flat.shape)

def reference(strain, seg_ids, dead, radius):
    seg_padded = jnp.pad(seg_ids, (MOST_REACH, MOST_REACH), constant_values=-1)
    segment_ids = jnp.arange(SEGMENTS, dtype=jnp.int32)
    dead_padded = lax.optimization_barrier(jnp.sum(jnp.where(seg_padded[:, None] == segment_ids[None, :], dead[None, :], 0), axis=1))
    alive_padded = jnp.where(seg_padded >= 0, 1 - dead_padded, 0)
    strain_wide = strain.astype(jnp.float32)
    padded = jnp.pad(strain_wide, ((MOST_REACH, MOST_REACH), (0, 0), (0, 0)))
    neighbor_sums = jnp.zeros(strain_wide.shape, jnp.float32)
    counts = jnp.zeros((CHANNELS,), jnp.float32)
    for offset in range(-MOST_REACH, MOST_REACH + 1):
        low_row = MOST_REACH + offset
        linked = (seg_padded[low_row:low_row + CHANNELS] == seg_ids) & (alive_padded[low_row:low_row + CHANNELS] > 0) & (abs(offset) <= radius)
        linked_f = linked.astype(jnp.float32)
        neighbor_sums = neighbor_sums + linked_f[:, None, None] * padded[low_row:low_row + CHANNELS]
        counts = counts + linked_f
    counts = jnp.maximum(counts, 1.0)
    alive_own = alive_padded[MOST_REACH:MOST_REACH + CHANNELS].astype(jnp.float32)
    filtered = alive_own[:, None, None] * (strain_wide - neighbor_sums / counts[:, None, None])
    spectra = jnp.dot(filtered.reshape(-1, SAMPLES), fourier_table(), precision=lax.Precision.HIGHEST)
    power_bins = spectra[:, :FREQ_BINS] ** 2 + spectra[:, FREQ_BINS:] ** 2
    smoothed = jnp.dot(power_bins, smoothing_table(), precision=lax.Precision.HIGHEST)
    inverse_amp = lax.rsqrt(jnp.maximum(smoothed, FLOOR_POWER))
    whitened = spectra * jnp.concatenate([inverse_amp, inverse_amp], axis=1)
    banded = whitened.reshape(CHANNELS, WINDOWS, 2, BANDS, BAND_BINS)
    inverse_count = 1.0 / (WINDOWS * BAND_BINS)

    def one_band(band):
        block_band = lax.dynamic_index_in_dim(banded, band, axis=3, keepdims=False).reshape(CHANNELS, -1)
        turned = swapped_parts(block_band, WINDOWS)
        real_part = jnp.dot(block_band, block_band.T, precision=lax.Precision.HIGHEST)
        real_part = (real_part * inverse_count).astype(jnp.bfloat16)
        imag_part = jnp.dot(block_band, turned.T, precision=lax.Precision.HIGHEST)
        imag_part = (imag_part * inverse_count).astype(jnp.bfloat16)
        return jnp.stack([real_part, imag_part], axis=0)
    return lax.map(one_band, jnp.arange(BANDS, dtype=jnp.int32))
```

```python
import numpy as np
import jax
import jax.numpy as jnp
from jax import lax
from jax.sharding import Mesh, PartitionSpec as P

SAMPLES = 1024
FREQ_BINS = 128
FIRST_BIN = 8
SMOOTH_BINS = 4
MOST_REACH = 8
ROW_GROUP = 8


FLOOR_POWER = 0.01

CHAN = ("ca", "cb")


def with_halo(x, width):
    devices, length = (lax.axis_size(CHAN), x.shape[0])
    up = [(i, (i + 1) % devices) for i in range(devices - 1)]
    down = [(j, i) for i, j in up]
    last = lax.slice_in_dim(x, length - width, length, axis=0)
    initial = lax.slice_in_dim(x, 0, width, axis=0)
    before = lax.ppermute(last, CHAN, up)
    after = lax.ppermute(initial, CHAN, down)
    return jnp.concatenate([before, x, after], axis=0)


def fourier_table():
    sample_ids = jnp.arange(SAMPLES, dtype=jnp.int32)
    bin_ids = FIRST_BIN + jnp.arange(FREQ_BINS, dtype=jnp.int32)
    phase_ids = sample_ids[:, None] * bin_ids[None, :] % SAMPLES
    angles = 2.0 * jnp.pi / SAMPLES * phase_ids.astype(jnp.float32)
    taper = 0.5 - 0.5 * jnp.cos(2.0 * jnp.pi / SAMPLES * (sample_ids.astype(jnp.float32) + 0.5))
    weights = taper[:, None] / jnp.sqrt(jnp.float32(SAMPLES))
    return jnp.concatenate([weights * jnp.cos(angles), -weights * jnp.sin(angles)], axis=1)


def smoothing_table():
    bin_ids = jnp.arange(FREQ_BINS, dtype=jnp.int32)
    nearby = (jnp.abs(bin_ids[:, None] - bin_ids[None, :]) <= SMOOTH_BINS).astype(jnp.float32)
    return nearby / jnp.sum(nearby, axis=0, keepdims=True)


def swapped_parts(flat, windows):
    parts = flat.reshape(flat.shape[:-1] + (windows, 2, -1))
    turned = jnp.stack([-parts[..., 1, :], parts[..., 0, :]], axis=-2)
    return turned.reshape(flat.shape)


def body(strain, seg_ids, dead, radius):
    local_rows = strain.shape[0]
    group_b = lax.axis_size("cb")
    group_a = lax.axis_size("ca")
    device = lax.axis_index("ca") * group_b + lax.axis_index("cb")
    seg_padded = jnp.pad(seg_ids, (MOST_REACH, MOST_REACH), constant_values=-1)
    near_segs = lax.dynamic_slice_in_dim(
        seg_padded, device * local_rows, local_rows + 2 * MOST_REACH
    )
    segment_ids = jnp.arange(dead.shape[0], dtype=jnp.int32)
    dead_near = jnp.sum(
        jnp.where(near_segs[:, None] == segment_ids[None, :], dead[None, :], 0), axis=1
    )
    alive_near = jnp.where(near_segs >= 0, 1 - dead_near, 0)
    own_segs = near_segs[MOST_REACH : MOST_REACH + local_rows]
    alive_own = alive_near[MOST_REACH : MOST_REACH + local_rows].astype(jnp.float32)
    columns = jnp.arange(local_rows + 2 * MOST_REACH, dtype=jnp.int32)[None, :]
    offsets = columns - (jnp.arange(local_rows, dtype=jnp.int32)[:, None] + MOST_REACH)
    linked = (
        (jnp.abs(offsets) <= radius[:, None])
        & (near_segs[None, :] == own_segs[:, None])
        & (alive_near[None, :] > 0)
    )
    linked_f = linked.astype(jnp.float32)
    counts = jnp.maximum(jnp.sum(linked_f, axis=1), 1.0)
    fourier = fourier_table()
    extended = with_halo(strain, MOST_REACH)
    neighbor_sums = jnp.einsum(
        "cr,rwt->cwt", linked.astype(jnp.bfloat16), extended, preferred_element_type=jnp.float32
    )
    filtered = alive_own[:, None, None] * (
        strain.astype(jnp.float32) - neighbor_sums / counts[:, None, None]
    )
    spectra = jnp.einsum("cwt,tk->cwk", filtered, fourier, precision=lax.Precision.HIGHEST)
    power_bins = spectra[..., :FREQ_BINS] ** 2 + spectra[..., FREQ_BINS:] ** 2
    smoothed = jnp.einsum(
        "cwk,kj->cwj", power_bins, smoothing_table(), precision=lax.Precision.HIGHEST
    )
    inverse_amp = lax.rsqrt(jnp.maximum(smoothed, FLOOR_POWER))
    whitened = spectra * jnp.concatenate([inverse_amp, inverse_amp], axis=-1)
    whitened = whitened.reshape(local_rows, strain.shape[1], 2, FREQ_BINS)
    banded = lax.all_to_all(whitened, "win", split_axis=3, concat_axis=1, tiled=True)
    windows = banded.shape[1]
    spectra_block = banded.reshape(local_rows, -1)
    inverse_count = 1.0 / (spectra_block.shape[1] // 2)
    row_set = lax.all_gather(spectra_block, "cb", axis=0, tiled=True)
    col_set = lax.all_gather(spectra_block, "ca", axis=0, tiled=True)
    operands = jnp.concatenate([col_set, swapped_parts(col_set, windows)], axis=0)
    product = jnp.einsum("ik,jk->ij", row_set, operands, precision=lax.Precision.HIGHEST)
    product = (product * inverse_count).astype(jnp.bfloat16)
    product = product.reshape(group_b * local_rows, 2, group_a, 1, local_rows)
    product = product.transpose(1, 0, 2, 3, 4)
    mine = lax.all_to_all(product, "cb", split_axis=1, concat_axis=3, tiled=True)
    cross_spectra = mine.reshape(2, local_rows, -1)
    return cross_spectra[None]


def solution(mesh):
    chan_size = mesh.shape["chan"]
    grid = mesh.devices.reshape(chan_size // ROW_GROUP, ROW_GROUP, mesh.shape["win"])
    sub_mesh = Mesh(grid, ("ca", "cb", "win"))
    return jax.shard_map(
        body,
        mesh=sub_mesh,
        in_specs=(P(CHAN, "win", None), P(), P(), P(CHAN)),
        out_specs=P("win", None, CHAN, None),
        check_vma=False,
    )
```

```python
import numpy as np
import jax
import jax.numpy as jnp
from jax import lax
from jax.sharding import Mesh, PartitionSpec as P

SAMPLES = 1024
FREQ_BINS = 128
FIRST_BIN = 8
SMOOTH_BINS = 4
MOST_REACH = 8
ROW_GROUP = 8


FLOOR_POWER = 0.01

CHAN = ("ca", "cb")


def with_halo(x, width):
    devices, length = (lax.axis_size(CHAN), x.shape[0])
    up = [(i, (i + 1) % devices) for i in range(devices - 1)]
    down = [(j, i) for i, j in up]
    last = lax.slice_in_dim(x, length - width, length, axis=0)
    initial = lax.slice_in_dim(x, 0, width, axis=0)
    before = lax.ppermute(last, CHAN, up)
    after = lax.ppermute(initial, CHAN, down)
    return jnp.concatenate([before, x, after], axis=0)


def gather_blocks(block, axis):
    size = lax.axis_size(axis)
    me = lax.axis_index(axis)
    pieces = [block]
    for shift in range(1, size):
        pairs = [(src, (src - shift) % size) for src in range(size)]
        pieces.append(lax.ppermute(block, axis, pairs))
    rel = jnp.concatenate(pieces + pieces, axis=0)
    rows = block.shape[0]
    start = ((size - me) % size) * rows
    return lax.dynamic_slice_in_dim(rel, start, size * rows, axis=0)


def fourier_table():
    sample_ids = jnp.arange(SAMPLES, dtype=jnp.int32)
    bin_ids = FIRST_BIN + jnp.arange(FREQ_BINS, dtype=jnp.int32)
    phase_ids = sample_ids[:, None] * bin_ids[None, :] % SAMPLES
    angles = 2.0 * jnp.pi / SAMPLES * phase_ids.astype(jnp.float32)
    taper = 0.5 - 0.5 * jnp.cos(2.0 * jnp.pi / SAMPLES * (sample_ids.astype(jnp.float32) + 0.5))
    weights = taper[:, None] / jnp.sqrt(jnp.float32(SAMPLES))
    return jnp.concatenate([weights * jnp.cos(angles), -weights * jnp.sin(angles)], axis=1)


def smoothing_table():
    bin_ids = jnp.arange(FREQ_BINS, dtype=jnp.int32)
    nearby = (jnp.abs(bin_ids[:, None] - bin_ids[None, :]) <= SMOOTH_BINS).astype(jnp.float32)
    return nearby / jnp.sum(nearby, axis=0, keepdims=True)


def swapped_parts(flat, windows):
    parts = flat.reshape(flat.shape[:-1] + (windows, 2, -1))
    turned = jnp.stack([-parts[..., 1, :], parts[..., 0, :]], axis=-2)
    return turned.reshape(flat.shape)


def body(strain, seg_ids, dead, radius):
    local_rows = strain.shape[0]
    group_b = lax.axis_size("cb")
    group_a = lax.axis_size("ca")
    device = lax.axis_index("ca") * group_b + lax.axis_index("cb")
    seg_padded = jnp.pad(seg_ids, (MOST_REACH, MOST_REACH), constant_values=-1)
    near_segs = lax.dynamic_slice_in_dim(
        seg_padded, device * local_rows, local_rows + 2 * MOST_REACH
    )
    segment_ids = jnp.arange(dead.shape[0], dtype=jnp.int32)
    dead_near = jnp.sum(
        jnp.where(near_segs[:, None] == segment_ids[None, :], dead[None, :], 0), axis=1
    )
    alive_near = jnp.where(near_segs >= 0, 1 - dead_near, 0)
    own_segs = near_segs[MOST_REACH : MOST_REACH + local_rows]
    alive_own = alive_near[MOST_REACH : MOST_REACH + local_rows].astype(jnp.float32)
    columns = jnp.arange(local_rows + 2 * MOST_REACH, dtype=jnp.int32)[None, :]
    offsets = columns - (jnp.arange(local_rows, dtype=jnp.int32)[:, None] + MOST_REACH)
    linked = (
        (jnp.abs(offsets) <= radius[:, None])
        & (near_segs[None, :] == own_segs[:, None])
        & (alive_near[None, :] > 0)
    )
    linked_f = linked.astype(jnp.float32)
    counts = jnp.maximum(jnp.sum(linked_f, axis=1), 1.0)
    fourier = fourier_table()
    extended = with_halo(strain, MOST_REACH)
    neighbor_sums = jnp.einsum(
        "cr,rwt->cwt", linked.astype(jnp.bfloat16), extended, preferred_element_type=jnp.float32
    )
    filtered = alive_own[:, None, None] * (
        strain.astype(jnp.float32) - neighbor_sums / counts[:, None, None]
    )
    spectra = jnp.einsum("cwt,tk->cwk", filtered, fourier, precision=lax.Precision.HIGHEST)
    power_bins = spectra[..., :FREQ_BINS] ** 2 + spectra[..., FREQ_BINS:] ** 2
    smoothed = jnp.einsum(
        "cwk,kj->cwj", power_bins, smoothing_table(), precision=lax.Precision.HIGHEST
    )
    inverse_amp = lax.rsqrt(jnp.maximum(smoothed, FLOOR_POWER))
    whitened = spectra * jnp.concatenate([inverse_amp, inverse_amp], axis=-1)
    whitened = whitened.reshape(local_rows, strain.shape[1], 2, FREQ_BINS)
    banded = lax.all_to_all(whitened, "win", split_axis=3, concat_axis=1, tiled=True)
    windows = banded.shape[1]
    spectra_block = banded.reshape(local_rows, -1)
    inverse_count = 1.0 / (spectra_block.shape[1] // 2)
    row_set = gather_blocks(spectra_block, "cb")
    col_set = gather_blocks(spectra_block, "ca")
    operands = jnp.concatenate([col_set, swapped_parts(col_set, windows)], axis=0)
    product = jnp.einsum("ik,jk->ij", row_set, operands, precision=lax.Precision.HIGHEST)
    product = (product * inverse_count).astype(jnp.bfloat16)
    product = product.reshape(group_b * local_rows, 2, group_a, local_rows)
    mine = lax.all_to_all(product, "cb", split_axis=0, concat_axis=0, tiled=True)
    mine = mine.reshape(group_b, local_rows, 2, group_a, local_rows)
    cross_spectra = mine.transpose(2, 1, 3, 0, 4).reshape(2, local_rows, -1)
    return cross_spectra[None]


def solution(mesh):
    chan_size = mesh.shape["chan"]
    grid = mesh.devices.reshape(chan_size // ROW_GROUP, ROW_GROUP, mesh.shape["win"])
    sub_mesh = Mesh(grid, ("ca", "cb", "win"))
    return jax.shard_map(
        body,
        mesh=sub_mesh,
        in_specs=(P(CHAN, "win", None), P(), P(), P(CHAN)),
        out_specs=P("win", None, CHAN, None),
        check_vma=False,
    )
```

```python
import numpy as np
import jax
import jax.numpy as jnp
from jax import lax
from jax.sharding import Mesh, PartitionSpec as P

SAMPLES = 1024
FREQ_BINS = 128
FIRST_BIN = 8
SMOOTH_BINS = 4
MOST_REACH = 8
ROW_GROUP = 8
COL_PAD = 128
ROW_PAD = 64


FLOOR_POWER = 0.01

CHAN = ("ca", "cb")


def with_halo(x, width):
    devices, length = (lax.axis_size(CHAN), x.shape[0])
    up = [(i, (i + 1) % devices) for i in range(devices - 1)]
    down = [(j, i) for i, j in up]
    last = lax.slice_in_dim(x, length - width, length, axis=0)
    initial = lax.slice_in_dim(x, 0, width, axis=0)
    before = lax.ppermute(last, CHAN, up)
    after = lax.ppermute(initial, CHAN, down)
    return jnp.concatenate([before, x, after], axis=0)


def gather_blocks(block, axis, padded_rows):
    rows = block.shape[0]
    wide = jnp.pad(block, ((0, padded_rows - rows), (0, 0)))
    every = lax.all_gather(wide, axis, axis=0, tiled=False)
    return every[:, :rows].reshape(-1, block.shape[1])

def fourier_table():
    sample_ids = jnp.arange(SAMPLES, dtype=jnp.int32)
    bin_ids = FIRST_BIN + jnp.arange(FREQ_BINS, dtype=jnp.int32)
    phase_ids = sample_ids[:, None] * bin_ids[None, :] % SAMPLES
    angles = 2.0 * jnp.pi / SAMPLES * phase_ids.astype(jnp.float32)
    taper = 0.5 - 0.5 * jnp.cos(2.0 * jnp.pi / SAMPLES * (sample_ids.astype(jnp.float32) + 0.5))
    weights = taper[:, None] / jnp.sqrt(jnp.float32(SAMPLES))
    return jnp.concatenate([weights * jnp.cos(angles), -weights * jnp.sin(angles)], axis=1)


def smoothing_table():
    bin_ids = jnp.arange(FREQ_BINS, dtype=jnp.int32)
    nearby = (jnp.abs(bin_ids[:, None] - bin_ids[None, :]) <= SMOOTH_BINS).astype(jnp.float32)
    return nearby / jnp.sum(nearby, axis=0, keepdims=True)


def swapped_parts(flat, windows):
    parts = flat.reshape(flat.shape[:-1] + (windows, 2, -1))
    turned = jnp.stack([-parts[..., 1, :], parts[..., 0, :]], axis=-2)
    return turned.reshape(flat.shape)


def body(strain, seg_ids, dead, radius):
    local_rows = strain.shape[0]
    group_b = lax.axis_size("cb")
    group_a = lax.axis_size("ca")
    device = lax.axis_index("ca") * group_b + lax.axis_index("cb")
    seg_padded = jnp.pad(seg_ids, (MOST_REACH, MOST_REACH), constant_values=-1)
    near_segs = lax.dynamic_slice_in_dim(
        seg_padded, device * local_rows, local_rows + 2 * MOST_REACH
    )
    segment_ids = jnp.arange(dead.shape[0], dtype=jnp.int32)
    dead_near = jnp.sum(
        jnp.where(near_segs[:, None] == segment_ids[None, :], dead[None, :], 0), axis=1
    )
    alive_near = jnp.where(near_segs >= 0, 1 - dead_near, 0)
    own_segs = near_segs[MOST_REACH : MOST_REACH + local_rows]
    alive_own = alive_near[MOST_REACH : MOST_REACH + local_rows].astype(jnp.float32)
    columns = jnp.arange(local_rows + 2 * MOST_REACH, dtype=jnp.int32)[None, :]
    offsets = columns - (jnp.arange(local_rows, dtype=jnp.int32)[:, None] + MOST_REACH)
    linked = (
        (jnp.abs(offsets) <= radius[:, None])
        & (near_segs[None, :] == own_segs[:, None])
        & (alive_near[None, :] > 0)
    )
    linked_f = linked.astype(jnp.float32)
    counts = jnp.maximum(jnp.sum(linked_f, axis=1), 1.0)
    fourier = fourier_table()
    extended = with_halo(strain, MOST_REACH)
    neighbor_sums = jnp.einsum(
        "cr,rwt->cwt", linked.astype(jnp.bfloat16), extended, preferred_element_type=jnp.float32
    )
    filtered = alive_own[:, None, None] * (
        strain.astype(jnp.float32) - neighbor_sums / counts[:, None, None]
    )
    spectra = jnp.einsum("cwt,tk->cwk", filtered, fourier, precision=lax.Precision.HIGHEST)
    power_bins = spectra[..., :FREQ_BINS] ** 2 + spectra[..., FREQ_BINS:] ** 2
    smoothed = jnp.einsum(
        "cwk,kj->cwj", power_bins, smoothing_table(), precision=lax.Precision.HIGHEST
    )
    inverse_amp = lax.rsqrt(jnp.maximum(smoothed, FLOOR_POWER))
    whitened = spectra * jnp.concatenate([inverse_amp, inverse_amp], axis=-1)
    whitened = whitened.reshape(local_rows, strain.shape[1], 2, FREQ_BINS)
    banded = lax.all_to_all(whitened, "win", split_axis=3, concat_axis=1, tiled=True)
    windows = banded.shape[1]
    spectra_block = banded.reshape(local_rows, -1)
    inverse_count = 1.0 / (spectra_block.shape[1] // 2)
    col_set = gather_blocks(spectra_block, "cb", COL_PAD)
    row_set = gather_blocks(spectra_block, "ca", ROW_PAD)
    operands = jnp.concatenate([col_set, swapped_parts(col_set, windows)], axis=0)
    product = jnp.einsum("ik,jk->ij", row_set, operands, precision=lax.Precision.HIGHEST)
    product = (product * inverse_count).astype(jnp.bfloat16)
    product = product.reshape(group_a, local_rows, operands.shape[0])
    mine = lax.all_to_all(product, "ca", split_axis=0, concat_axis=0, tiled=True)
    mine = mine.reshape(group_a, local_rows, 2, col_set.shape[0])
    cross_spectra = mine.transpose(2, 1, 0, 3).reshape(2, local_rows, -1)
    return cross_spectra[None]


def solution(mesh):
    chan_size = mesh.shape["chan"]
    grid = mesh.devices.reshape(chan_size // ROW_GROUP, ROW_GROUP, mesh.shape["win"])
    sub_mesh = Mesh(grid, ("ca", "cb", "win"))
    return jax.shard_map(
        body,
        mesh=sub_mesh,
        in_specs=(P(CHAN, "win", None), P(), P(), P(CHAN)),
        out_specs=P("win", None, CHAN, None),
        check_vma=False,
    )
```

```python
import numpy as np
import jax
import jax.numpy as jnp
from jax import lax
from jax.sharding import Mesh, PartitionSpec as P

SAMPLES = 1024
FREQ_BINS = 128
FIRST_BIN = 8
SMOOTH_BINS = 4
MOST_REACH = 8
ROW_GROUP = 8


FLOOR_POWER = 0.01

CHAN = ("ca", "cb")


def with_halo(x, width):
    devices, length = (lax.axis_size(CHAN), x.shape[0])
    up = [(i, (i + 1) % devices) for i in range(devices - 1)]
    down = [(j, i) for i, j in up]
    last = lax.slice_in_dim(x, length - width, length, axis=0)
    initial = lax.slice_in_dim(x, 0, width, axis=0)
    before = lax.ppermute(last, CHAN, up)
    after = lax.ppermute(initial, CHAN, down)
    return jnp.concatenate([before, x, after], axis=0)


def gather_blocks(block, axis):
    size = lax.axis_size(axis)
    copies = jnp.broadcast_to(block[None], (size,) + block.shape)
    every = lax.all_to_all(copies, axis, split_axis=0, concat_axis=0, tiled=True)
    return every.reshape(-1, block.shape[1])

def fourier_table():
    sample_ids = jnp.arange(SAMPLES, dtype=jnp.int32)
    bin_ids = FIRST_BIN + jnp.arange(FREQ_BINS, dtype=jnp.int32)
    phase_ids = sample_ids[:, None] * bin_ids[None, :] % SAMPLES
    angles = 2.0 * jnp.pi / SAMPLES * phase_ids.astype(jnp.float32)
    taper = 0.5 - 0.5 * jnp.cos(2.0 * jnp.pi / SAMPLES * (sample_ids.astype(jnp.float32) + 0.5))
    weights = taper[:, None] / jnp.sqrt(jnp.float32(SAMPLES))
    return jnp.concatenate([weights * jnp.cos(angles), -weights * jnp.sin(angles)], axis=1)


def smoothing_table():
    bin_ids = jnp.arange(FREQ_BINS, dtype=jnp.int32)
    nearby = (jnp.abs(bin_ids[:, None] - bin_ids[None, :]) <= SMOOTH_BINS).astype(jnp.float32)
    return nearby / jnp.sum(nearby, axis=0, keepdims=True)


def swapped_parts(flat, windows):
    parts = flat.reshape(flat.shape[:-1] + (windows, 2, -1))
    turned = jnp.stack([-parts[..., 1, :], parts[..., 0, :]], axis=-2)
    return turned.reshape(flat.shape)


def body(strain, seg_ids, dead, radius):
    local_rows = strain.shape[0]
    group_b = lax.axis_size("cb")
    group_a = lax.axis_size("ca")
    device = lax.axis_index("ca") * group_b + lax.axis_index("cb")
    seg_padded = jnp.pad(seg_ids, (MOST_REACH, MOST_REACH), constant_values=-1)
    near_segs = lax.dynamic_slice_in_dim(
        seg_padded, device * local_rows, local_rows + 2 * MOST_REACH
    )
    segment_ids = jnp.arange(dead.shape[0], dtype=jnp.int32)
    dead_near = jnp.sum(
        jnp.where(near_segs[:, None] == segment_ids[None, :], dead[None, :], 0), axis=1
    )
    alive_near = jnp.where(near_segs >= 0, 1 - dead_near, 0)
    own_segs = near_segs[MOST_REACH : MOST_REACH + local_rows]
    alive_own = alive_near[MOST_REACH : MOST_REACH + local_rows].astype(jnp.float32)
    columns = jnp.arange(local_rows + 2 * MOST_REACH, dtype=jnp.int32)[None, :]
    offsets = columns - (jnp.arange(local_rows, dtype=jnp.int32)[:, None] + MOST_REACH)
    linked = (
        (jnp.abs(offsets) <= radius[:, None])
        & (near_segs[None, :] == own_segs[:, None])
        & (alive_near[None, :] > 0)
    )
    linked_f = linked.astype(jnp.float32)
    counts = jnp.maximum(jnp.sum(linked_f, axis=1), 1.0)
    fourier = fourier_table()
    extended = with_halo(strain, MOST_REACH)
    neighbor_sums = jnp.einsum(
        "cr,rwt->cwt", linked.astype(jnp.bfloat16), extended, preferred_element_type=jnp.float32
    )
    filtered = alive_own[:, None, None] * (
        strain.astype(jnp.float32) - neighbor_sums / counts[:, None, None]
    )
    spectra = jnp.einsum("cwt,tk->cwk", filtered, fourier, precision=lax.Precision.HIGHEST)
    power_bins = spectra[..., :FREQ_BINS] ** 2 + spectra[..., FREQ_BINS:] ** 2
    smoothed = jnp.einsum(
        "cwk,kj->cwj", power_bins, smoothing_table(), precision=lax.Precision.HIGHEST
    )
    inverse_amp = lax.rsqrt(jnp.maximum(smoothed, FLOOR_POWER))
    whitened = spectra * jnp.concatenate([inverse_amp, inverse_amp], axis=-1)
    whitened = whitened.reshape(local_rows, strain.shape[1], 2, FREQ_BINS)
    banded = lax.all_to_all(whitened, "win", split_axis=3, concat_axis=1, tiled=True)
    windows = banded.shape[1]
    spectra_block = banded.reshape(local_rows, -1)
    inverse_count = 1.0 / (spectra_block.shape[1] // 2)
    col_set = gather_blocks(spectra_block, "cb")
    row_set = gather_blocks(spectra_block, "ca")
    operands = jnp.concatenate([col_set, swapped_parts(col_set, windows)], axis=0)
    product = jnp.einsum("ik,jk->ij", row_set, operands, precision=lax.Precision.HIGHEST)
    product = (product * inverse_count).astype(jnp.bfloat16)
    product = product.reshape(group_a, local_rows, operands.shape[0])
    mine = lax.all_to_all(product, "ca", split_axis=0, concat_axis=0, tiled=True)
    mine = mine.reshape(group_a, local_rows, 2, col_set.shape[0])
    cross_spectra = mine.transpose(2, 1, 0, 3).reshape(2, local_rows, -1)
    return cross_spectra[None]


def solution(mesh):
    chan_size = mesh.shape["chan"]
    grid = mesh.devices.reshape(chan_size // ROW_GROUP, ROW_GROUP, mesh.shape["win"])
    sub_mesh = Mesh(grid, ("ca", "cb", "win"))
    return jax.shard_map(
        body,
        mesh=sub_mesh,
        in_specs=(P(CHAN, "win", None), P(), P(), P(CHAN)),
        out_specs=P("win", None, CHAN, None),
        check_vma=False,
    )
```

```python
import numpy as np
import jax
import jax.numpy as jnp
from jax import lax
from jax.sharding import Mesh, PartitionSpec as P

SAMPLES = 1024
FREQ_BINS = 128
FIRST_BIN = 8
SMOOTH_BINS = 4
MOST_REACH = 8
ROW_GROUP = 8


FLOOR_POWER = 0.01

CHAN = ("ca", "cb")


def with_halo(x, width):
    devices, length = (lax.axis_size(CHAN), x.shape[0])
    up = [(i, (i + 1) % devices) for i in range(devices - 1)]
    down = [(j, i) for i, j in up]
    last = lax.slice_in_dim(x, length - width, length, axis=0)
    initial = lax.slice_in_dim(x, 0, width, axis=0)
    before = lax.ppermute(last, CHAN, up)
    after = lax.ppermute(initial, CHAN, down)
    return jnp.concatenate([before, x, after], axis=0)


def gather_blocks(block, axis):
    size = lax.axis_size(axis)
    copies = jnp.broadcast_to(block[None], (size,) + block.shape)
    every = lax.all_to_all(copies, axis, split_axis=0, concat_axis=0, tiled=True)
    return every.reshape(-1, block.shape[1])

def fourier_table():
    sample_ids = jnp.arange(SAMPLES, dtype=jnp.int32)
    bin_ids = FIRST_BIN + jnp.arange(FREQ_BINS, dtype=jnp.int32)
    phase_ids = sample_ids[:, None] * bin_ids[None, :] % SAMPLES
    angles = 2.0 * jnp.pi / SAMPLES * phase_ids.astype(jnp.float32)
    taper = 0.5 - 0.5 * jnp.cos(2.0 * jnp.pi / SAMPLES * (sample_ids.astype(jnp.float32) + 0.5))
    weights = taper[:, None] / jnp.sqrt(jnp.float32(SAMPLES))
    return jnp.concatenate([weights * jnp.cos(angles), -weights * jnp.sin(angles)], axis=1)


def smoothing_table():
    bin_ids = jnp.arange(FREQ_BINS, dtype=jnp.int32)
    nearby = (jnp.abs(bin_ids[:, None] - bin_ids[None, :]) <= SMOOTH_BINS).astype(jnp.float32)
    return nearby / jnp.sum(nearby, axis=0, keepdims=True)


def swapped_parts(flat, windows):
    parts = flat.reshape(flat.shape[:-1] + (windows, 2, -1))
    turned = jnp.stack([-parts[..., 1, :], parts[..., 0, :]], axis=-2)
    return turned.reshape(flat.shape)


def body(strain, seg_ids, dead, radius):
    local_rows = strain.shape[0]
    group_b = lax.axis_size("cb")
    group_a = lax.axis_size("ca")
    device = lax.axis_index("ca") * group_b + lax.axis_index("cb")
    seg_padded = jnp.pad(seg_ids, (MOST_REACH, MOST_REACH), constant_values=-1)
    near_segs = lax.dynamic_slice_in_dim(
        seg_padded, device * local_rows, local_rows + 2 * MOST_REACH
    )
    segment_ids = jnp.arange(dead.shape[0], dtype=jnp.int32)
    dead_near = jnp.sum(
        jnp.where(near_segs[:, None] == segment_ids[None, :], dead[None, :], 0), axis=1
    )
    alive_near = jnp.where(near_segs >= 0, 1 - dead_near, 0)
    own_segs = near_segs[MOST_REACH : MOST_REACH + local_rows]
    alive_own = alive_near[MOST_REACH : MOST_REACH + local_rows].astype(jnp.float32)
    columns = jnp.arange(local_rows + 2 * MOST_REACH, dtype=jnp.int32)[None, :]
    offsets = columns - (jnp.arange(local_rows, dtype=jnp.int32)[:, None] + MOST_REACH)
    linked = (
        (jnp.abs(offsets) <= radius[:, None])
        & (near_segs[None, :] == own_segs[:, None])
        & (alive_near[None, :] > 0)
    )
    linked_f = linked.astype(jnp.float32)
    counts = jnp.maximum(jnp.sum(linked_f, axis=1), 1.0)
    fourier = fourier_table()
    extended = with_halo(strain, MOST_REACH)
    neighbor_sums = jnp.einsum(
        "cr,rwt->cwt", linked.astype(jnp.bfloat16), extended, preferred_element_type=jnp.float32
    )
    filtered = alive_own[:, None, None] * (
        strain.astype(jnp.float32) - neighbor_sums / counts[:, None, None]
    )
    spectra = jnp.einsum("cwt,tk->cwk", filtered, fourier, precision=lax.Precision.HIGHEST)
    power_bins = spectra[..., :FREQ_BINS] ** 2 + spectra[..., FREQ_BINS:] ** 2
    smoothed = jnp.einsum(
        "cwk,kj->cwj", power_bins, smoothing_table(), precision=lax.Precision.HIGHEST
    )
    inverse_amp = lax.rsqrt(jnp.maximum(smoothed, FLOOR_POWER))
    whitened = spectra * jnp.concatenate([inverse_amp, inverse_amp], axis=-1)
    whitened = whitened.reshape(local_rows, strain.shape[1], 2, FREQ_BINS)
    banded = lax.all_to_all(whitened, "win", split_axis=3, concat_axis=1, tiled=True)
    windows = banded.shape[1]
    spectra_block = banded.reshape(local_rows, -1)
    inverse_count = 1.0 / (spectra_block.shape[1] // 2)
    chan_size = group_a * group_b
    pairs = [((dst % group_b) * group_a + dst // group_b, dst) for dst in range(chan_size)]
    placed = lax.ppermute(spectra_block, CHAN, pairs)
    row_set = gather_blocks(spectra_block, "cb")
    col_set = gather_blocks(placed, "ca")
    operands = jnp.concatenate([col_set, swapped_parts(col_set, windows)], axis=0)
    product = jnp.einsum("ik,jk->ij", row_set, operands, precision=lax.Precision.HIGHEST)
    product = (product * inverse_count).astype(jnp.bfloat16)
    product = product.reshape(group_b, local_rows, operands.shape[0])
    mine = lax.all_to_all(product, "cb", split_axis=0, concat_axis=0, tiled=True)
    mine = mine.reshape(group_b, local_rows, 2, col_set.shape[0])
    cross_spectra = mine.transpose(2, 1, 0, 3).reshape(2, local_rows, -1)
    return cross_spectra[None]


def solution(mesh):
    chan_size = mesh.shape["chan"]
    grid = mesh.devices.reshape(chan_size // ROW_GROUP, ROW_GROUP, mesh.shape["win"])
    sub_mesh = Mesh(grid, ("ca", "cb", "win"))
    return jax.shard_map(
        body,
        mesh=sub_mesh,
        in_specs=(P(CHAN, "win", None), P(), P(), P(CHAN)),
        out_specs=P("win", None, CHAN, None),
        check_vma=False,
    )
```

```python
import numpy as np
import jax
import jax.numpy as jnp
from jax import lax
from jax.sharding import Mesh, PartitionSpec as P

SAMPLES = 1024
FREQ_BINS = 128
FIRST_BIN = 8
SMOOTH_BINS = 4
MOST_REACH = 8
ROW_GROUP = 8
Z_GROUP = 4


FLOOR_POWER = 0.01

CHAN = ("cx", "cz", "cb")


def with_halo(x, width):
    devices, length = (lax.axis_size(CHAN), x.shape[0])
    up = [(i, (i + 1) % devices) for i in range(devices - 1)]
    down = [(j, i) for i, j in up]
    last = lax.slice_in_dim(x, length - width, length, axis=0)
    initial = lax.slice_in_dim(x, 0, width, axis=0)
    before = lax.ppermute(last, CHAN, up)
    after = lax.ppermute(initial, CHAN, down)
    return jnp.concatenate([before, x, after], axis=0)


def gather_blocks(block, axis):
    size = lax.axis_size(axis)
    copies = jnp.broadcast_to(block[None], (size,) + block.shape)
    every = lax.all_to_all(copies, axis, split_axis=0, concat_axis=0, tiled=True)
    return every.reshape(-1, block.shape[1])

def fourier_table():
    sample_ids = jnp.arange(SAMPLES, dtype=jnp.int32)
    bin_ids = FIRST_BIN + jnp.arange(FREQ_BINS, dtype=jnp.int32)
    phase_ids = sample_ids[:, None] * bin_ids[None, :] % SAMPLES
    angles = 2.0 * jnp.pi / SAMPLES * phase_ids.astype(jnp.float32)
    taper = 0.5 - 0.5 * jnp.cos(2.0 * jnp.pi / SAMPLES * (sample_ids.astype(jnp.float32) + 0.5))
    weights = taper[:, None] / jnp.sqrt(jnp.float32(SAMPLES))
    return jnp.concatenate([weights * jnp.cos(angles), -weights * jnp.sin(angles)], axis=1)


def smoothing_table():
    bin_ids = jnp.arange(FREQ_BINS, dtype=jnp.int32)
    nearby = (jnp.abs(bin_ids[:, None] - bin_ids[None, :]) <= SMOOTH_BINS).astype(jnp.float32)
    return nearby / jnp.sum(nearby, axis=0, keepdims=True)


def swapped_parts(flat, windows):
    parts = flat.reshape(flat.shape[:-1] + (windows, 2, -1))
    turned = jnp.stack([-parts[..., 1, :], parts[..., 0, :]], axis=-2)
    return turned.reshape(flat.shape)


def body(strain, seg_ids, dead, radius):
    local_rows = strain.shape[0]
    group_b = lax.axis_size("cb")
    group_x = lax.axis_size("cx")
    group_z = lax.axis_size("cz")
    device = (lax.axis_index("cx") * group_z + lax.axis_index("cz")) * group_b + lax.axis_index("cb")
    seg_padded = jnp.pad(seg_ids, (MOST_REACH, MOST_REACH), constant_values=-1)
    near_segs = lax.dynamic_slice_in_dim(
        seg_padded, device * local_rows, local_rows + 2 * MOST_REACH
    )
    segment_ids = jnp.arange(dead.shape[0], dtype=jnp.int32)
    dead_near = jnp.sum(
        jnp.where(near_segs[:, None] == segment_ids[None, :], dead[None, :], 0), axis=1
    )
    alive_near = jnp.where(near_segs >= 0, 1 - dead_near, 0)
    own_segs = near_segs[MOST_REACH : MOST_REACH + local_rows]
    alive_own = alive_near[MOST_REACH : MOST_REACH + local_rows].astype(jnp.float32)
    columns = jnp.arange(local_rows + 2 * MOST_REACH, dtype=jnp.int32)[None, :]
    offsets = columns - (jnp.arange(local_rows, dtype=jnp.int32)[:, None] + MOST_REACH)
    linked = (
        (jnp.abs(offsets) <= radius[:, None])
        & (near_segs[None, :] == own_segs[:, None])
        & (alive_near[None, :] > 0)
    )
    linked_f = linked.astype(jnp.float32)
    counts = jnp.maximum(jnp.sum(linked_f, axis=1), 1.0)
    fourier = fourier_table()
    extended = with_halo(strain, MOST_REACH)
    neighbor_sums = jnp.einsum(
        "cr,rwt->cwt", linked.astype(jnp.bfloat16), extended, preferred_element_type=jnp.float32
    )
    filtered = alive_own[:, None, None] * (
        strain.astype(jnp.float32) - neighbor_sums / counts[:, None, None]
    )
    spectra = jnp.einsum("cwt,tk->cwk", filtered, fourier, precision=lax.Precision.HIGHEST)
    power_bins = spectra[..., :FREQ_BINS] ** 2 + spectra[..., FREQ_BINS:] ** 2
    smoothed = jnp.einsum(
        "cwk,kj->cwj", power_bins, smoothing_table(), precision=lax.Precision.HIGHEST
    )
    inverse_amp = lax.rsqrt(jnp.maximum(smoothed, FLOOR_POWER))
    whitened = spectra * jnp.concatenate([inverse_amp, inverse_amp], axis=-1)
    whitened = whitened.reshape(local_rows, strain.shape[1], 2, FREQ_BINS)
    banded = lax.all_to_all(whitened, "win", split_axis=3, concat_axis=1, tiled=True)
    windows = banded.shape[1]
    spectra_block = banded.reshape(local_rows, -1)
    inverse_count = 1.0 / (spectra_block.shape[1] // 2)
    col_set = gather_blocks(spectra_block, "cb")
    row_set = gather_blocks(gather_blocks(spectra_block, "cz"), "cx")
    operands = jnp.concatenate([col_set, swapped_parts(col_set, windows)], axis=0)
    product = jnp.einsum("ik,jk->ij", row_set, operands, precision=lax.Precision.HIGHEST)
    product = (product * inverse_count).astype(jnp.bfloat16)
    product = product.reshape(group_x, group_z, local_rows, operands.shape[0])
    stage = lax.all_to_all(product, "cx", split_axis=0, concat_axis=0, tiled=True)
    stage = stage.transpose(1, 0, 2, 3)
    mine = lax.all_to_all(stage, "cz", split_axis=0, concat_axis=0, tiled=True)
    mine = mine.reshape(group_z, group_x, local_rows, 2, col_set.shape[0])
    cross_spectra = mine.transpose(3, 2, 1, 0, 4).reshape(2, local_rows, -1)
    return cross_spectra[None]


def solution(mesh):
    chan_size = mesh.shape["chan"]
    outer = chan_size // ROW_GROUP
    grid = mesh.devices.reshape(outer // Z_GROUP, Z_GROUP, ROW_GROUP, mesh.shape["win"])
    sub_mesh = Mesh(grid, ("cx", "cz", "cb", "win"))
    return jax.shard_map(
        body,
        mesh=sub_mesh,
        in_specs=(P(CHAN, "win", None), P(), P(), P(CHAN)),
        out_specs=P("win", None, CHAN, None),
        check_vma=False,
    )
```

```python
import numpy as np
import jax
import jax.numpy as jnp
from jax import lax
from jax.sharding import Mesh, PartitionSpec as P

SAMPLES = 1024
FREQ_BINS = 128
FIRST_BIN = 8
SMOOTH_BINS = 4
MOST_REACH = 8
ROW_GROUP = 8
COL_PAD = 128


FLOOR_POWER = 0.01

CHAN = ("ca", "cb")


def with_halo(x, width):
    devices, length = (lax.axis_size(CHAN), x.shape[0])
    up = [(i, (i + 1) % devices) for i in range(devices - 1)]
    down = [(j, i) for i, j in up]
    last = lax.slice_in_dim(x, length - width, length, axis=0)
    initial = lax.slice_in_dim(x, 0, width, axis=0)
    before = lax.ppermute(last, CHAN, up)
    after = lax.ppermute(initial, CHAN, down)
    return jnp.concatenate([before, x, after], axis=0)


def gather_blocks(block, axis):
    size = lax.axis_size(axis)
    copies = jnp.broadcast_to(block[None], (size,) + block.shape)
    every = lax.all_to_all(copies, axis, split_axis=0, concat_axis=0, tiled=True)
    return every.reshape(-1, block.shape[1])

def gather_offloaded(block, axis, padded_rows):
    rows = block.shape[0]
    wide = jnp.pad(block, ((0, padded_rows - rows), (0, 0)))
    every = lax.all_gather(wide, axis, axis=0, tiled=False)
    return every[:, :rows].reshape(-1, block.shape[1])

def fourier_table():
    sample_ids = jnp.arange(SAMPLES, dtype=jnp.int32)
    bin_ids = FIRST_BIN + jnp.arange(FREQ_BINS, dtype=jnp.int32)
    phase_ids = sample_ids[:, None] * bin_ids[None, :] % SAMPLES
    angles = 2.0 * jnp.pi / SAMPLES * phase_ids.astype(jnp.float32)
    taper = 0.5 - 0.5 * jnp.cos(2.0 * jnp.pi / SAMPLES * (sample_ids.astype(jnp.float32) + 0.5))
    weights = taper[:, None] / jnp.sqrt(jnp.float32(SAMPLES))
    return jnp.concatenate([weights * jnp.cos(angles), -weights * jnp.sin(angles)], axis=1)


def smoothing_table():
    bin_ids = jnp.arange(FREQ_BINS, dtype=jnp.int32)
    nearby = (jnp.abs(bin_ids[:, None] - bin_ids[None, :]) <= SMOOTH_BINS).astype(jnp.float32)
    return nearby / jnp.sum(nearby, axis=0, keepdims=True)


def swapped_parts(flat, windows):
    parts = flat.reshape(flat.shape[:-1] + (windows, 2, -1))
    turned = jnp.stack([-parts[..., 1, :], parts[..., 0, :]], axis=-2)
    return turned.reshape(flat.shape)


def body(strain, seg_ids, dead, radius):
    local_rows = strain.shape[0]
    group_b = lax.axis_size("cb")
    group_a = lax.axis_size("ca")
    device = lax.axis_index("ca") * group_b + lax.axis_index("cb")
    seg_padded = jnp.pad(seg_ids, (MOST_REACH, MOST_REACH), constant_values=-1)
    near_segs = lax.dynamic_slice_in_dim(
        seg_padded, device * local_rows, local_rows + 2 * MOST_REACH
    )
    segment_ids = jnp.arange(dead.shape[0], dtype=jnp.int32)
    dead_near = jnp.sum(
        jnp.where(near_segs[:, None] == segment_ids[None, :], dead[None, :], 0), axis=1
    )
    alive_near = jnp.where(near_segs >= 0, 1 - dead_near, 0)
    own_segs = near_segs[MOST_REACH : MOST_REACH + local_rows]
    alive_own = alive_near[MOST_REACH : MOST_REACH + local_rows].astype(jnp.float32)
    columns = jnp.arange(local_rows + 2 * MOST_REACH, dtype=jnp.int32)[None, :]
    offsets = columns - (jnp.arange(local_rows, dtype=jnp.int32)[:, None] + MOST_REACH)
    linked = (
        (jnp.abs(offsets) <= radius[:, None])
        & (near_segs[None, :] == own_segs[:, None])
        & (alive_near[None, :] > 0)
    )
    linked_f = linked.astype(jnp.float32)
    counts = jnp.maximum(jnp.sum(linked_f, axis=1), 1.0)
    fourier = fourier_table()
    extended = with_halo(strain, MOST_REACH)
    neighbor_sums = jnp.einsum(
        "cr,rwt->cwt", linked.astype(jnp.bfloat16), extended, preferred_element_type=jnp.float32
    )
    filtered = alive_own[:, None, None] * (
        strain.astype(jnp.float32) - neighbor_sums / counts[:, None, None]
    )
    spectra = jnp.einsum("cwt,tk->cwk", filtered, fourier, precision=lax.Precision.HIGHEST)
    power_bins = spectra[..., :FREQ_BINS] ** 2 + spectra[..., FREQ_BINS:] ** 2
    smoothed = jnp.einsum(
        "cwk,kj->cwj", power_bins, smoothing_table(), precision=lax.Precision.HIGHEST
    )
    inverse_amp = lax.rsqrt(jnp.maximum(smoothed, FLOOR_POWER))
    whitened = spectra * jnp.concatenate([inverse_amp, inverse_amp], axis=-1)
    whitened = whitened.reshape(local_rows, strain.shape[1], 2, FREQ_BINS)
    banded = lax.all_to_all(whitened, "win", split_axis=3, concat_axis=1, tiled=True)
    windows = banded.shape[1]
    spectra_block = banded.reshape(local_rows, -1)
    inverse_count = 1.0 / (spectra_block.shape[1] // 2)
    col_set = gather_offloaded(spectra_block, "cb", COL_PAD)
    row_set = gather_blocks(spectra_block, "ca")
    operands = jnp.concatenate([col_set, swapped_parts(col_set, windows)], axis=0)
    product = jnp.einsum("ik,jk->ij", row_set, operands, precision=lax.Precision.HIGHEST)
    product = (product * inverse_count).astype(jnp.bfloat16)
    product = product.reshape(group_a, local_rows, operands.shape[0])
    mine = lax.all_to_all(product, "ca", split_axis=0, concat_axis=0, tiled=True)
    mine = mine.reshape(group_a, local_rows, 2, col_set.shape[0])
    cross_spectra = mine.transpose(2, 1, 0, 3).reshape(2, local_rows, -1)
    return cross_spectra[None]


def solution(mesh):
    chan_size = mesh.shape["chan"]
    grid = mesh.devices.reshape(chan_size // ROW_GROUP, ROW_GROUP, mesh.shape["win"])
    sub_mesh = Mesh(grid, ("ca", "cb", "win"))
    return jax.shard_map(
        body,
        mesh=sub_mesh,
        in_specs=(P(CHAN, "win", None), P(), P(), P(CHAN)),
        out_specs=P("win", None, CHAN, None),
        check_vma=False,
    )
```

```python
import numpy as np
import jax
import jax.numpy as jnp
from jax import lax
from jax.sharding import Mesh, PartitionSpec as P

SAMPLES = 1024
FREQ_BINS = 128
FIRST_BIN = 8
SMOOTH_BINS = 4
MOST_REACH = 8
ROW_GROUP = 8
Z_GROUP = 4


FLOOR_POWER = 0.01

CHAN = ("cx", "cz", "cb")


def with_halo(x, width):
    devices, length = (lax.axis_size(CHAN), x.shape[0])
    up = [(i, (i + 1) % devices) for i in range(devices - 1)]
    down = [(j, i) for i, j in up]
    last = lax.slice_in_dim(x, length - width, length, axis=0)
    initial = lax.slice_in_dim(x, 0, width, axis=0)
    before = lax.ppermute(last, CHAN, up)
    after = lax.ppermute(initial, CHAN, down)
    return jnp.concatenate([before, x, after], axis=0)


def gather_blocks(block, axis):
    size = lax.axis_size(axis)
    copies = jnp.broadcast_to(block[None], (size,) + block.shape)
    every = lax.all_to_all(copies, axis, split_axis=0, concat_axis=0, tiled=True)
    return every.reshape(-1, block.shape[1])

def fourier_table():
    sample_ids = jnp.arange(SAMPLES, dtype=jnp.int32)
    bin_ids = FIRST_BIN + jnp.arange(FREQ_BINS, dtype=jnp.int32)
    phase_ids = sample_ids[:, None] * bin_ids[None, :] % SAMPLES
    angles = 2.0 * jnp.pi / SAMPLES * phase_ids.astype(jnp.float32)
    taper = 0.5 - 0.5 * jnp.cos(2.0 * jnp.pi / SAMPLES * (sample_ids.astype(jnp.float32) + 0.5))
    weights = taper[:, None] / jnp.sqrt(jnp.float32(SAMPLES))
    return jnp.concatenate([weights * jnp.cos(angles), -weights * jnp.sin(angles)], axis=1)


def smoothing_table():
    bin_ids = jnp.arange(FREQ_BINS, dtype=jnp.int32)
    nearby = (jnp.abs(bin_ids[:, None] - bin_ids[None, :]) <= SMOOTH_BINS).astype(jnp.float32)
    return nearby / jnp.sum(nearby, axis=0, keepdims=True)


def swapped_parts(flat, windows):
    parts = flat.reshape(flat.shape[:-1] + (windows, 2, -1))
    turned = jnp.stack([-parts[..., 1, :], parts[..., 0, :]], axis=-2)
    return turned.reshape(flat.shape)


def body(strain, seg_ids, dead, radius):
    local_rows = strain.shape[0]
    group_b = lax.axis_size("cb")
    group_x = lax.axis_size("cx")
    group_z = lax.axis_size("cz")
    device = (lax.axis_index("cx") * group_z + lax.axis_index("cz")) * group_b + lax.axis_index("cb")
    seg_padded = jnp.pad(seg_ids, (MOST_REACH, MOST_REACH), constant_values=-1)
    near_segs = lax.dynamic_slice_in_dim(
        seg_padded, device * local_rows, local_rows + 2 * MOST_REACH
    )
    segment_ids = jnp.arange(dead.shape[0], dtype=jnp.int32)
    dead_near = jnp.sum(
        jnp.where(near_segs[:, None] == segment_ids[None, :], dead[None, :], 0), axis=1
    )
    alive_near = jnp.where(near_segs >= 0, 1 - dead_near, 0)
    own_segs = near_segs[MOST_REACH : MOST_REACH + local_rows]
    alive_own = alive_near[MOST_REACH : MOST_REACH + local_rows].astype(jnp.float32)
    columns = jnp.arange(local_rows + 2 * MOST_REACH, dtype=jnp.int32)[None, :]
    offsets = columns - (jnp.arange(local_rows, dtype=jnp.int32)[:, None] + MOST_REACH)
    linked = (
        (jnp.abs(offsets) <= radius[:, None])
        & (near_segs[None, :] == own_segs[:, None])
        & (alive_near[None, :] > 0)
    )
    linked_f = linked.astype(jnp.float32)
    counts = jnp.maximum(jnp.sum(linked_f, axis=1), 1.0)
    fourier = fourier_table()
    extended = with_halo(strain, MOST_REACH)
    neighbor_sums = jnp.einsum(
        "cr,rwt->cwt", linked.astype(jnp.bfloat16), extended, preferred_element_type=jnp.float32
    )
    filtered = alive_own[:, None, None] * (
        strain.astype(jnp.float32) - neighbor_sums / counts[:, None, None]
    )
    spectra = jnp.einsum("cwt,tk->cwk", filtered, fourier, precision=lax.Precision.HIGHEST)
    power_bins = spectra[..., :FREQ_BINS] ** 2 + spectra[..., FREQ_BINS:] ** 2
    smoothed = jnp.einsum(
        "cwk,kj->cwj", power_bins, smoothing_table(), precision=lax.Precision.HIGHEST
    )
    inverse_amp = lax.rsqrt(jnp.maximum(smoothed, FLOOR_POWER))
    whitened = spectra * jnp.concatenate([inverse_amp, inverse_amp], axis=-1)
    whitened = whitened.reshape(local_rows, strain.shape[1], 2, FREQ_BINS)
    banded = lax.all_to_all(whitened, "win", split_axis=3, concat_axis=1, tiled=True)
    windows = banded.shape[1]
    spectra_block = banded.reshape(local_rows, -1)
    inverse_count = 1.0 / (spectra_block.shape[1] // 2)
    col_set = gather_blocks(gather_blocks(spectra_block, "cb"), "cz")
    row_set = gather_blocks(spectra_block, "cx")
    operands = jnp.concatenate([col_set, swapped_parts(col_set, windows)], axis=0)
    product = jnp.einsum("ik,jk->ij", row_set, operands, precision=lax.Precision.HIGHEST)
    product = (product * inverse_count).astype(jnp.bfloat16)
    product = product.reshape(group_x, local_rows, operands.shape[0])
    mine = lax.all_to_all(product, "cx", split_axis=0, concat_axis=0, tiled=True)
    mine = mine.reshape(group_x, local_rows, 2, col_set.shape[0])
    cross_spectra = mine.transpose(2, 1, 0, 3).reshape(2, local_rows, -1)
    return cross_spectra[None]


def solution(mesh):
    chan_size = mesh.shape["chan"]
    outer = chan_size // ROW_GROUP
    grid = mesh.devices.reshape(outer // Z_GROUP, Z_GROUP, ROW_GROUP, mesh.shape["win"])
    sub_mesh = Mesh(grid, ("cx", "cz", "cb", "win"))
    return jax.shard_map(
        body,
        mesh=sub_mesh,
        in_specs=(P(CHAN, "win", None), P(), P(), P(CHAN)),
        out_specs=P("win", None, CHAN, None),
        check_vma=False,
    )
```

```python
import numpy as np
import jax
import jax.numpy as jnp
from jax import lax
from jax.sharding import Mesh, PartitionSpec as P

SAMPLES = 1024
FREQ_BINS = 128
FIRST_BIN = 8
SMOOTH_BINS = 4
MOST_REACH = 8
ROW_GROUP = 8
Z_GROUP = 4


FLOOR_POWER = 0.01

CHAN = ("cx", "cz", "cb")


def with_halo(x, width):
    devices, length = (lax.axis_size(CHAN), x.shape[0])
    up = [(i, (i + 1) % devices) for i in range(devices - 1)]
    down = [(j, i) for i, j in up]
    last = lax.slice_in_dim(x, length - width, length, axis=0)
    initial = lax.slice_in_dim(x, 0, width, axis=0)
    before = lax.ppermute(last, CHAN, up)
    after = lax.ppermute(initial, CHAN, down)
    return jnp.concatenate([before, x, after], axis=0)


def gather_blocks(block, axis):
    size = lax.axis_size(axis)
    copies = jnp.broadcast_to(block[None], (size,) + block.shape)
    every = lax.all_to_all(copies, axis, split_axis=0, concat_axis=0, tiled=True)
    return every.reshape(-1, block.shape[1])

def fourier_table():
    sample_ids = jnp.arange(SAMPLES, dtype=jnp.int32)
    bin_ids = FIRST_BIN + jnp.arange(FREQ_BINS, dtype=jnp.int32)
    phase_ids = sample_ids[:, None] * bin_ids[None, :] % SAMPLES
    angles = 2.0 * jnp.pi / SAMPLES * phase_ids.astype(jnp.float32)
    taper = 0.5 - 0.5 * jnp.cos(2.0 * jnp.pi / SAMPLES * (sample_ids.astype(jnp.float32) + 0.5))
    weights = taper[:, None] / jnp.sqrt(jnp.float32(SAMPLES))
    return jnp.concatenate([weights * jnp.cos(angles), -weights * jnp.sin(angles)], axis=1)


def smoothing_table():
    bin_ids = jnp.arange(FREQ_BINS, dtype=jnp.int32)
    nearby = (jnp.abs(bin_ids[:, None] - bin_ids[None, :]) <= SMOOTH_BINS).astype(jnp.float32)
    return nearby / jnp.sum(nearby, axis=0, keepdims=True)


def swapped_parts(flat, windows):
    parts = flat.reshape(flat.shape[:-1] + (windows, 2, -1))
    turned = jnp.stack([-parts[..., 1, :], parts[..., 0, :]], axis=-2)
    return turned.reshape(flat.shape)


def body(strain, seg_ids, dead, radius):
    local_rows = strain.shape[0]
    group_b = lax.axis_size("cb")
    group_x = lax.axis_size("cx")
    group_z = lax.axis_size("cz")
    device = (lax.axis_index("cx") * group_z + lax.axis_index("cz")) * group_b + lax.axis_index("cb")
    seg_padded = jnp.pad(seg_ids, (MOST_REACH, MOST_REACH), constant_values=-1)
    near_segs = lax.dynamic_slice_in_dim(
        seg_padded, device * local_rows, local_rows + 2 * MOST_REACH
    )
    segment_ids = jnp.arange(dead.shape[0], dtype=jnp.int32)
    dead_near = jnp.sum(
        jnp.where(near_segs[:, None] == segment_ids[None, :], dead[None, :], 0), axis=1
    )
    alive_near = jnp.where(near_segs >= 0, 1 - dead_near, 0)
    own_segs = near_segs[MOST_REACH : MOST_REACH + local_rows]
    alive_own = alive_near[MOST_REACH : MOST_REACH + local_rows].astype(jnp.float32)
    columns = jnp.arange(local_rows + 2 * MOST_REACH, dtype=jnp.int32)[None, :]
    offsets = columns - (jnp.arange(local_rows, dtype=jnp.int32)[:, None] + MOST_REACH)
    linked = (
        (jnp.abs(offsets) <= radius[:, None])
        & (near_segs[None, :] == own_segs[:, None])
        & (alive_near[None, :] > 0)
    )
    linked_f = linked.astype(jnp.float32)
    counts = jnp.maximum(jnp.sum(linked_f, axis=1), 1.0)
    fourier = fourier_table()
    extended = with_halo(strain, MOST_REACH)
    neighbor_sums = jnp.einsum(
        "cr,rwt->cwt", linked.astype(jnp.bfloat16), extended, preferred_element_type=jnp.float32
    )
    filtered = alive_own[:, None, None] * (
        strain.astype(jnp.float32) - neighbor_sums / counts[:, None, None]
    )
    spectra = jnp.einsum("cwt,tk->cwk", filtered, fourier, precision=lax.Precision.HIGHEST)
    power_bins = spectra[..., :FREQ_BINS] ** 2 + spectra[..., FREQ_BINS:] ** 2
    smoothed = jnp.einsum(
        "cwk,kj->cwj", power_bins, smoothing_table(), precision=lax.Precision.HIGHEST
    )
    inverse_amp = lax.rsqrt(jnp.maximum(smoothed, FLOOR_POWER))
    whitened = spectra * jnp.concatenate([inverse_amp, inverse_amp], axis=-1)
    whitened = whitened.reshape(local_rows, strain.shape[1], 2, FREQ_BINS)
    banded = lax.all_to_all(whitened, "win", split_axis=3, concat_axis=1, tiled=True)
    windows = banded.shape[1]
    spectra_block = banded.reshape(local_rows, -1)
    inverse_count = 1.0 / (spectra_block.shape[1] // 2)
    col_set = gather_blocks(gather_blocks(spectra_block, "cz"), "cb")
    col_set = col_set.reshape(group_b, group_z, local_rows, -1).transpose(1, 0, 2, 3)
    col_set = col_set.reshape(group_z * group_b * local_rows, -1)
    row_set = gather_blocks(spectra_block, "cx")
    operands = jnp.concatenate([col_set, swapped_parts(col_set, windows)], axis=0)
    product = jnp.einsum("ik,jk->ij", row_set, operands, precision=lax.Precision.HIGHEST)
    product = (product * inverse_count).astype(jnp.bfloat16)
    product = product.reshape(group_x, local_rows, operands.shape[0])
    mine = lax.all_to_all(product, "cx", split_axis=0, concat_axis=0, tiled=True)
    mine = mine.reshape(group_x, local_rows, 2, col_set.shape[0])
    cross_spectra = mine.transpose(2, 1, 0, 3).reshape(2, local_rows, -1)
    return cross_spectra[None]


def solution(mesh):
    chan_size = mesh.shape["chan"]
    outer = chan_size // ROW_GROUP
    grid = mesh.devices.reshape(outer // Z_GROUP, Z_GROUP, ROW_GROUP, mesh.shape["win"])
    sub_mesh = Mesh(grid, ("cx", "cz", "cb", "win"))
    return jax.shard_map(
        body,
        mesh=sub_mesh,
        in_specs=(P(CHAN, "win", None), P(), P(), P(CHAN)),
        out_specs=P("win", None, CHAN, None),
        check_vma=False,
    )
```

```python
import numpy as np
import jax
import jax.numpy as jnp
from jax import lax
from jax.sharding import Mesh, PartitionSpec as P

SAMPLES = 1024
FREQ_BINS = 128
FIRST_BIN = 8
SMOOTH_BINS = 4
MOST_REACH = 8
ROW_GROUP = 8
Z_GROUP = 4


FLOOR_POWER = 0.01

CHAN = ("cx", "cz", "cb")


def with_halo(x, width):
    devices, length = (lax.axis_size(CHAN), x.shape[0])
    up = [(i, (i + 1) % devices) for i in range(devices - 1)]
    down = [(j, i) for i, j in up]
    last = lax.slice_in_dim(x, length - width, length, axis=0)
    initial = lax.slice_in_dim(x, 0, width, axis=0)
    before = lax.ppermute(last, CHAN, up)
    after = lax.ppermute(initial, CHAN, down)
    return jnp.concatenate([before, x, after], axis=0)


def gather_blocks(block, axis):
    size = lax.axis_size(axis)
    copies = jnp.broadcast_to(block[None], (size,) + block.shape)
    every = lax.all_to_all(copies, axis, split_axis=0, concat_axis=0, tiled=True)
    return every.reshape(-1, block.shape[1])

def fourier_table():
    sample_ids = np.arange(SAMPLES)
    bin_ids = FIRST_BIN + np.arange(FREQ_BINS)
    angles = 2.0 * np.pi / SAMPLES * (sample_ids[:, None] * bin_ids[None, :] % SAMPLES)
    taper = 0.5 - 0.5 * np.cos(2.0 * np.pi / SAMPLES * (sample_ids + 0.5))
    weights = taper[:, None] / np.sqrt(SAMPLES)
    table = np.concatenate([weights * np.cos(angles), -weights * np.sin(angles)], axis=1)
    return jnp.asarray(table.astype(np.float32))


def smoothing_table():
    bin_ids = jnp.arange(FREQ_BINS, dtype=jnp.int32)
    nearby = (jnp.abs(bin_ids[:, None] - bin_ids[None, :]) <= SMOOTH_BINS).astype(jnp.float32)
    return nearby / jnp.sum(nearby, axis=0, keepdims=True)


def swapped_parts(flat, windows):
    parts = flat.reshape(flat.shape[:-1] + (windows, 2, -1))
    turned = jnp.stack([-parts[..., 1, :], parts[..., 0, :]], axis=-2)
    return turned.reshape(flat.shape)


def body(strain, seg_ids, dead, radius):
    local_rows = strain.shape[0]
    group_b = lax.axis_size("cb")
    group_x = lax.axis_size("cx")
    group_z = lax.axis_size("cz")
    device = (lax.axis_index("cx") * group_z + lax.axis_index("cz")) * group_b + lax.axis_index("cb")
    seg_padded = jnp.pad(seg_ids, (MOST_REACH, MOST_REACH), constant_values=-1)
    near_segs = lax.dynamic_slice_in_dim(
        seg_padded, device * local_rows, local_rows + 2 * MOST_REACH
    )
    segment_ids = jnp.arange(dead.shape[0], dtype=jnp.int32)
    dead_near = jnp.sum(
        jnp.where(near_segs[:, None] == segment_ids[None, :], dead[None, :], 0), axis=1
    )
    alive_near = jnp.where(near_segs >= 0, 1 - dead_near, 0)
    own_segs = near_segs[MOST_REACH : MOST_REACH + local_rows]
    alive_own = alive_near[MOST_REACH : MOST_REACH + local_rows].astype(jnp.float32)
    columns = jnp.arange(local_rows + 2 * MOST_REACH, dtype=jnp.int32)[None, :]
    offsets = columns - (jnp.arange(local_rows, dtype=jnp.int32)[:, None] + MOST_REACH)
    linked = (
        (jnp.abs(offsets) <= radius[:, None])
        & (near_segs[None, :] == own_segs[:, None])
        & (alive_near[None, :] > 0)
    )
    linked_f = linked.astype(jnp.float32)
    counts = jnp.maximum(jnp.sum(linked_f, axis=1), 1.0)
    fourier = fourier_table()
    extended = with_halo(strain, MOST_REACH)
    neighbor_sums = jnp.einsum(
        "cr,rwt->cwt", linked.astype(jnp.bfloat16), extended, preferred_element_type=jnp.float32
    )
    filtered = alive_own[:, None, None] * (
        strain.astype(jnp.float32) - neighbor_sums / counts[:, None, None]
    )
    spectra = jnp.einsum("cwt,tk->cwk", filtered, fourier, precision=lax.Precision.HIGHEST)
    power_bins = spectra[..., :FREQ_BINS] ** 2 + spectra[..., FREQ_BINS:] ** 2
    smoothed = jnp.einsum(
        "cwk,kj->cwj", power_bins, smoothing_table(), precision=lax.Precision.HIGHEST
    )
    inverse_amp = lax.rsqrt(jnp.maximum(smoothed, FLOOR_POWER))
    whitened = spectra * jnp.concatenate([inverse_amp, inverse_amp], axis=-1)
    whitened = whitened.reshape(local_rows, strain.shape[1], 2, FREQ_BINS)
    banded = lax.all_to_all(whitened, "win", split_axis=3, concat_axis=1, tiled=True)
    windows = banded.shape[1]
    spectra_block = banded.reshape(local_rows, -1)
    inverse_count = 1.0 / (spectra_block.shape[1] // 2)
    col_set = gather_blocks(spectra_block, "cb")
    row_set = gather_blocks(gather_blocks(spectra_block, "cz"), "cx")
    operands = jnp.concatenate([col_set, swapped_parts(col_set, windows)], axis=0)
    product = jnp.einsum("ik,jk->ij", row_set, operands, precision=lax.Precision.HIGHEST)
    product = (product * inverse_count).astype(jnp.bfloat16)
    product = product.reshape(group_x * group_z, local_rows, operands.shape[0])
    mine = lax.all_to_all(product, ("cx", "cz"), split_axis=0, concat_axis=0, tiled=True)
    mine = mine.reshape(group_x * group_z, local_rows, 2, col_set.shape[0])
    cross_spectra = mine.transpose(2, 1, 0, 3).reshape(2, local_rows, -1)
    return cross_spectra[None]


def solution(mesh):
    chan_size = mesh.shape["chan"]
    outer = chan_size // ROW_GROUP
    grid = mesh.devices.reshape(outer // Z_GROUP, Z_GROUP, ROW_GROUP, mesh.shape["win"])
    sub_mesh = Mesh(grid, ("cx", "cz", "cb", "win"))
    return jax.shard_map(
        body,
        mesh=sub_mesh,
        in_specs=(P(CHAN, "win", None), P(), P(), P(CHAN)),
        out_specs=P("win", None, CHAN, None),
        check_vma=False,
    )
```

```python
import numpy as np
import jax
import jax.numpy as jnp
from jax import lax
from jax.sharding import Mesh, PartitionSpec as P

SAMPLES = 1024
FREQ_BINS = 128
FIRST_BIN = 8
SMOOTH_BINS = 4
MOST_REACH = 8
ROW_GROUP = 8
Z_GROUP = 4


FLOOR_POWER = 0.01

CHAN = ("cx", "cz", "cb")


def with_halo(x, width):
    devices, length = (lax.axis_size(CHAN), x.shape[0])
    up = [(i, (i + 1) % devices) for i in range(devices - 1)]
    down = [(j, i) for i, j in up]
    last = lax.slice_in_dim(x, length - width, length, axis=0)
    initial = lax.slice_in_dim(x, 0, width, axis=0)
    before = lax.ppermute(last, CHAN, up)
    after = lax.ppermute(initial, CHAN, down)
    return jnp.concatenate([before, x, after], axis=0)


def gather_blocks(block, axis):
    size = lax.axis_size(axis)
    copies = jnp.broadcast_to(block[None], (size,) + block.shape)
    every = lax.all_to_all(copies, axis, split_axis=0, concat_axis=0, tiled=True)
    return every.reshape(-1, block.shape[1])

def spread_band(per_band, axis):
    size = lax.axis_size(axis)
    bands, rows, width = per_band.shape
    copies = jnp.broadcast_to(per_band[None], (size, bands, rows, width)).reshape(size * bands, rows, width)
    every = lax.all_to_all(copies, (axis, "win"), split_axis=0, concat_axis=0, tiled=True)
    every = every.reshape(size, bands, rows, width).transpose(0, 2, 1, 3)
    return every.reshape(size * rows, bands * width)

def fourier_table():
    sample_ids = np.arange(SAMPLES)
    bin_ids = FIRST_BIN + np.arange(FREQ_BINS)
    angles = 2.0 * np.pi / SAMPLES * (sample_ids[:, None] * bin_ids[None, :] % SAMPLES)
    taper = 0.5 - 0.5 * np.cos(2.0 * np.pi / SAMPLES * (sample_ids + 0.5))
    weights = taper[:, None] / np.sqrt(SAMPLES)
    table = np.concatenate([weights * np.cos(angles), -weights * np.sin(angles)], axis=1)
    return jnp.asarray(table.astype(np.float32))


def smoothing_table():
    bin_ids = jnp.arange(FREQ_BINS, dtype=jnp.int32)
    nearby = (jnp.abs(bin_ids[:, None] - bin_ids[None, :]) <= SMOOTH_BINS).astype(jnp.float32)
    return nearby / jnp.sum(nearby, axis=0, keepdims=True)


def swapped_parts(flat, windows):
    parts = flat.reshape(flat.shape[:-1] + (windows, 2, -1))
    turned = jnp.stack([-parts[..., 1, :], parts[..., 0, :]], axis=-2)
    return turned.reshape(flat.shape)


def body(strain, seg_ids, dead, radius):
    local_rows = strain.shape[0]
    group_b = lax.axis_size("cb")
    group_x = lax.axis_size("cx")
    group_z = lax.axis_size("cz")
    device = (lax.axis_index("cx") * group_z + lax.axis_index("cz")) * group_b + lax.axis_index("cb")
    seg_padded = jnp.pad(seg_ids, (MOST_REACH, MOST_REACH), constant_values=-1)
    near_segs = lax.dynamic_slice_in_dim(
        seg_padded, device * local_rows, local_rows + 2 * MOST_REACH
    )
    segment_ids = jnp.arange(dead.shape[0], dtype=jnp.int32)
    dead_near = jnp.sum(
        jnp.where(near_segs[:, None] == segment_ids[None, :], dead[None, :], 0), axis=1
    )
    alive_near = jnp.where(near_segs >= 0, 1 - dead_near, 0)
    own_segs = near_segs[MOST_REACH : MOST_REACH + local_rows]
    alive_own = alive_near[MOST_REACH : MOST_REACH + local_rows].astype(jnp.float32)
    columns = jnp.arange(local_rows + 2 * MOST_REACH, dtype=jnp.int32)[None, :]
    offsets = columns - (jnp.arange(local_rows, dtype=jnp.int32)[:, None] + MOST_REACH)
    linked = (
        (jnp.abs(offsets) <= radius[:, None])
        & (near_segs[None, :] == own_segs[:, None])
        & (alive_near[None, :] > 0)
    )
    linked_f = linked.astype(jnp.float32)
    counts = jnp.maximum(jnp.sum(linked_f, axis=1), 1.0)
    fourier = fourier_table()
    extended = with_halo(strain, MOST_REACH)
    neighbor_sums = jnp.einsum(
        "cr,rwt->cwt", linked.astype(jnp.bfloat16), extended, preferred_element_type=jnp.float32
    )
    filtered = alive_own[:, None, None] * (
        strain.astype(jnp.float32) - neighbor_sums / counts[:, None, None]
    )
    spectra = jnp.einsum("cwt,tk->cwk", filtered, fourier, precision=lax.Precision.HIGHEST)
    power_bins = spectra[..., :FREQ_BINS] ** 2 + spectra[..., FREQ_BINS:] ** 2
    smoothed = jnp.einsum(
        "cwk,kj->cwj", power_bins, smoothing_table(), precision=lax.Precision.HIGHEST
    )
    inverse_amp = lax.rsqrt(jnp.maximum(smoothed, FLOOR_POWER))
    whitened = spectra * jnp.concatenate([inverse_amp, inverse_amp], axis=-1)
    bands = lax.axis_size("win")
    whitened = whitened.reshape(local_rows, 2, bands, FREQ_BINS // bands).transpose(2, 0, 1, 3)
    whitened = whitened.reshape(bands, local_rows, -1)
    windows = bands
    inverse_count = 1.0 / (windows * whitened.shape[2] // 2)
    col_set = spread_band(whitened, "cb")
    row_set = gather_blocks(spread_band(whitened, "cz"), "cx")
    operands = jnp.concatenate([col_set, swapped_parts(col_set, windows)], axis=0)
    product = jnp.einsum("ik,jk->ij", row_set, operands, precision=lax.Precision.HIGHEST)
    product = (product * inverse_count).astype(jnp.bfloat16)
    product = product.reshape(group_x * group_z, local_rows, operands.shape[0])
    mine = lax.all_to_all(product, ("cx", "cz"), split_axis=0, concat_axis=0, tiled=True)
    mine = mine.reshape(group_x * group_z, local_rows, 2, col_set.shape[0])
    cross_spectra = mine.transpose(2, 1, 0, 3).reshape(2, local_rows, -1)
    return cross_spectra[None]


def solution(mesh):
    chan_size = mesh.shape["chan"]
    outer = chan_size // ROW_GROUP
    grid = mesh.devices.reshape(outer // Z_GROUP, Z_GROUP, ROW_GROUP, mesh.shape["win"])
    sub_mesh = Mesh(grid, ("cx", "cz", "cb", "win"))
    return jax.shard_map(
        body,
        mesh=sub_mesh,
        in_specs=(P(CHAN, "win", None), P(), P(), P(CHAN)),
        out_specs=P("win", None, CHAN, None),
        check_vma=False,
    )
```

```python
import numpy as np
import jax
import jax.numpy as jnp
from jax import lax
from jax.sharding import Mesh, PartitionSpec as P

SAMPLES = 1024
FREQ_BINS = 128
FIRST_BIN = 8
SMOOTH_BINS = 4
MOST_REACH = 8
ROW_GROUP = 8
Z_GROUP = 4


FLOOR_POWER = 0.01

CHAN = ("cx", "cz", "cb")


def with_halo(x, width):
    devices, length = (lax.axis_size(CHAN), x.shape[0])
    up = [(i, (i + 1) % devices) for i in range(devices - 1)]
    down = [(j, i) for i, j in up]
    last = lax.slice_in_dim(x, length - width, length, axis=0)
    initial = lax.slice_in_dim(x, 0, width, axis=0)
    before = lax.ppermute(last, CHAN, up)
    after = lax.ppermute(initial, CHAN, down)
    return jnp.concatenate([before, x, after], axis=0)


def gather_blocks(block, axis):
    size = lax.axis_size(axis)
    copies = jnp.broadcast_to(block[None], (size,) + block.shape)
    every = lax.all_to_all(copies, axis, split_axis=0, concat_axis=0, tiled=True)
    return every.reshape(-1, block.shape[1])

def spread_band(per_band, axes):
    size = lax.axis_size(axes)
    bands, rows, width = per_band.shape
    copies = jnp.broadcast_to(per_band[None], (size, bands, rows, width)).reshape(size * bands, rows, width)
    every = lax.all_to_all(copies, axes + ("win",), split_axis=0, concat_axis=0, tiled=True)
    every = every.reshape(size, bands, rows, width).transpose(0, 2, 1, 3)
    return every.reshape(size * rows, bands * width)

def fourier_table():
    sample_ids = np.arange(SAMPLES)
    bin_ids = FIRST_BIN + np.arange(FREQ_BINS)
    angles = 2.0 * np.pi / SAMPLES * (sample_ids[:, None] * bin_ids[None, :] % SAMPLES)
    taper = 0.5 - 0.5 * np.cos(2.0 * np.pi / SAMPLES * (sample_ids + 0.5))
    weights = taper[:, None] / np.sqrt(SAMPLES)
    table = np.concatenate([weights * np.cos(angles), -weights * np.sin(angles)], axis=1)
    return jnp.asarray(table.astype(np.float32))


def smoothing_table():
    bin_ids = jnp.arange(FREQ_BINS, dtype=jnp.int32)
    nearby = (jnp.abs(bin_ids[:, None] - bin_ids[None, :]) <= SMOOTH_BINS).astype(jnp.float32)
    return nearby / jnp.sum(nearby, axis=0, keepdims=True)


def swapped_parts(flat, windows):
    parts = flat.reshape(flat.shape[:-1] + (windows, 2, -1))
    turned = jnp.stack([-parts[..., 1, :], parts[..., 0, :]], axis=-2)
    return turned.reshape(flat.shape)


def body(strain, seg_ids, dead, radius):
    local_rows = strain.shape[0]
    group_b = lax.axis_size("cb")
    group_x = lax.axis_size("cx")
    group_z = lax.axis_size("cz")
    device = (lax.axis_index("cx") * group_z + lax.axis_index("cz")) * group_b + lax.axis_index("cb")
    seg_padded = jnp.pad(seg_ids, (MOST_REACH, MOST_REACH), constant_values=-1)
    near_segs = lax.dynamic_slice_in_dim(
        seg_padded, device * local_rows, local_rows + 2 * MOST_REACH
    )
    segment_ids = jnp.arange(dead.shape[0], dtype=jnp.int32)
    dead_near = jnp.sum(
        jnp.where(near_segs[:, None] == segment_ids[None, :], dead[None, :], 0), axis=1
    )
    alive_near = jnp.where(near_segs >= 0, 1 - dead_near, 0)
    own_segs = near_segs[MOST_REACH : MOST_REACH + local_rows]
    alive_own = alive_near[MOST_REACH : MOST_REACH + local_rows].astype(jnp.float32)
    columns = jnp.arange(local_rows + 2 * MOST_REACH, dtype=jnp.int32)[None, :]
    offsets = columns - (jnp.arange(local_rows, dtype=jnp.int32)[:, None] + MOST_REACH)
    linked = (
        (jnp.abs(offsets) <= radius[:, None])
        & (near_segs[None, :] == own_segs[:, None])
        & (alive_near[None, :] > 0)
    )
    linked_f = linked.astype(jnp.float32)
    counts = jnp.maximum(jnp.sum(linked_f, axis=1), 1.0)
    fourier = fourier_table()
    extended = with_halo(strain, MOST_REACH)
    neighbor_sums = jnp.einsum(
        "cr,rwt->cwt", linked.astype(jnp.bfloat16), extended, preferred_element_type=jnp.float32
    )
    filtered = alive_own[:, None, None] * (
        strain.astype(jnp.float32) - neighbor_sums / counts[:, None, None]
    )
    spectra = jnp.einsum("cwt,tk->cwk", filtered, fourier, precision=lax.Precision.HIGHEST)
    power_bins = spectra[..., :FREQ_BINS] ** 2 + spectra[..., FREQ_BINS:] ** 2
    smoothed = jnp.einsum(
        "cwk,kj->cwj", power_bins, smoothing_table(), precision=lax.Precision.HIGHEST
    )
    inverse_amp = lax.rsqrt(jnp.maximum(smoothed, FLOOR_POWER))
    whitened = spectra * jnp.concatenate([inverse_amp, inverse_amp], axis=-1)
    bands = lax.axis_size("win")
    whitened = whitened.reshape(local_rows, 2, bands, FREQ_BINS // bands).transpose(2, 0, 1, 3)
    whitened = whitened.reshape(bands, local_rows, -1)
    windows = bands
    inverse_count = 1.0 / (windows * whitened.shape[2] // 2)
    col_set = spread_band(whitened, ("cb",))
    row_set = spread_band(whitened, ("cx", "cz"))
    operands = jnp.concatenate([col_set, swapped_parts(col_set, windows)], axis=0)
    product = jnp.einsum("ik,jk->ij", row_set, operands, precision=lax.Precision.HIGH)
    product = (product * inverse_count).astype(jnp.bfloat16)
    product = product.reshape(group_x * group_z, local_rows, operands.shape[0])
    mine = lax.all_to_all(product, ("cx", "cz"), split_axis=0, concat_axis=0, tiled=True)
    mine = mine.reshape(group_x * group_z, local_rows, 2, col_set.shape[0])
    cross_spectra = mine.transpose(2, 1, 0, 3).reshape(2, local_rows, -1)
    return cross_spectra[None]


def solution(mesh):
    chan_size = mesh.shape["chan"]
    outer = chan_size // ROW_GROUP
    grid = mesh.devices.reshape(outer // Z_GROUP, Z_GROUP, ROW_GROUP, mesh.shape["win"])
    sub_mesh = Mesh(grid, ("cx", "cz", "cb", "win"))
    return jax.shard_map(
        body,
        mesh=sub_mesh,
        in_specs=(P(CHAN, "win", None), P(), P(), P(CHAN)),
        out_specs=P("win", None, CHAN, None),
        check_vma=False,
    )
```

```python
import numpy as np
import jax
import jax.numpy as jnp
from jax import lax
from jax.sharding import Mesh, PartitionSpec as P

SAMPLES = 1024
FREQ_BINS = 128
FIRST_BIN = 8
SMOOTH_BINS = 4
MOST_REACH = 8
ROW_GROUP = 8
Z_GROUP = 4


FLOOR_POWER = 0.01

CHAN = ("cx", "cz", "cb")


def with_halo(x, width):
    devices, length = (lax.axis_size(CHAN), x.shape[0])
    up = [(i, (i + 1) % devices) for i in range(devices - 1)]
    down = [(j, i) for i, j in up]
    last = lax.slice_in_dim(x, length - width, length, axis=0)
    initial = lax.slice_in_dim(x, 0, width, axis=0)
    before = lax.ppermute(last, CHAN, up)
    after = lax.ppermute(initial, CHAN, down)
    return jnp.concatenate([before, x, after], axis=0)


def gather_blocks(block, axis):
    size = lax.axis_size(axis)
    copies = jnp.broadcast_to(block[None], (size,) + block.shape)
    every = lax.all_to_all(copies, axis, split_axis=0, concat_axis=0, tiled=True)
    return every.reshape(-1, block.shape[1])

def spread_band(per_band, axis):
    size = lax.axis_size(axis)
    bands, rows, width = per_band.shape
    copies = jnp.broadcast_to(per_band[None], (size, bands, rows, width)).reshape(size * bands, rows, width)
    every = lax.all_to_all(copies, (axis, "win"), split_axis=0, concat_axis=0, tiled=True)
    every = every.reshape(size, bands, rows, width).transpose(0, 2, 1, 3)
    return every.reshape(size * rows, bands * width)

def gather_by_permutes(block, axis):
    size = lax.axis_size(axis)
    me = lax.axis_index(axis)
    pieces = [block]
    for shift in range(1, size):
        pairs = [(src, (src - shift) % size) for src in range(size)]
        pieces.append(lax.ppermute(block, axis, pairs))
    rel = jnp.concatenate(pieces + pieces, axis=0)
    rows = block.shape[0]
    start = ((size - me) % size) * rows
    return lax.dynamic_slice_in_dim(rel, start, size * rows, axis=0)

def fourier_table():
    sample_ids = np.arange(SAMPLES)
    bin_ids = FIRST_BIN + np.arange(FREQ_BINS)
    angles = 2.0 * np.pi / SAMPLES * (sample_ids[:, None] * bin_ids[None, :] % SAMPLES)
    taper = 0.5 - 0.5 * np.cos(2.0 * np.pi / SAMPLES * (sample_ids + 0.5))
    weights = taper[:, None] / np.sqrt(SAMPLES)
    table = np.concatenate([weights * np.cos(angles), -weights * np.sin(angles)], axis=1)
    return jnp.asarray(table.astype(np.float32))


def smoothing_table():
    bin_ids = jnp.arange(FREQ_BINS, dtype=jnp.int32)
    nearby = (jnp.abs(bin_ids[:, None] - bin_ids[None, :]) <= SMOOTH_BINS).astype(jnp.float32)
    return nearby / jnp.sum(nearby, axis=0, keepdims=True)


def swapped_parts(flat, windows):
    parts = flat.reshape(flat.shape[:-1] + (windows, 2, -1))
    turned = jnp.stack([-parts[..., 1, :], parts[..., 0, :]], axis=-2)
    return turned.reshape(flat.shape)


def body(strain, seg_ids, dead, radius):
    local_rows = strain.shape[0]
    group_b = lax.axis_size("cb")
    group_x = lax.axis_size("cx")
    group_z = lax.axis_size("cz")
    device = (lax.axis_index("cx") * group_z + lax.axis_index("cz")) * group_b + lax.axis_index("cb")
    seg_padded = jnp.pad(seg_ids, (MOST_REACH, MOST_REACH), constant_values=-1)
    near_segs = lax.dynamic_slice_in_dim(
        seg_padded, device * local_rows, local_rows + 2 * MOST_REACH
    )
    segment_ids = jnp.arange(dead.shape[0], dtype=jnp.int32)
    dead_near = jnp.sum(
        jnp.where(near_segs[:, None] == segment_ids[None, :], dead[None, :], 0), axis=1
    )
    alive_near = jnp.where(near_segs >= 0, 1 - dead_near, 0)
    own_segs = near_segs[MOST_REACH : MOST_REACH + local_rows]
    alive_own = alive_near[MOST_REACH : MOST_REACH + local_rows].astype(jnp.float32)
    columns = jnp.arange(local_rows + 2 * MOST_REACH, dtype=jnp.int32)[None, :]
    offsets = columns - (jnp.arange(local_rows, dtype=jnp.int32)[:, None] + MOST_REACH)
    linked = (
        (jnp.abs(offsets) <= radius[:, None])
        & (near_segs[None, :] == own_segs[:, None])
        & (alive_near[None, :] > 0)
    )
    linked_f = linked.astype(jnp.float32)
    counts = jnp.maximum(jnp.sum(linked_f, axis=1), 1.0)
    fourier = fourier_table()
    extended = with_halo(strain, MOST_REACH)
    neighbor_sums = jnp.einsum(
        "cr,rwt->cwt", linked.astype(jnp.bfloat16), extended, preferred_element_type=jnp.float32
    )
    filtered = alive_own[:, None, None] * (
        strain.astype(jnp.float32) - neighbor_sums / counts[:, None, None]
    )
    spectra = jnp.einsum("cwt,tk->cwk", filtered, fourier, precision=lax.Precision.HIGHEST)
    power_bins = spectra[..., :FREQ_BINS] ** 2 + spectra[..., FREQ_BINS:] ** 2
    smoothed = jnp.einsum(
        "cwk,kj->cwj", power_bins, smoothing_table(), precision=lax.Precision.HIGHEST
    )
    inverse_amp = lax.rsqrt(jnp.maximum(smoothed, FLOOR_POWER))
    whitened = spectra * jnp.concatenate([inverse_amp, inverse_amp], axis=-1)
    bands = lax.axis_size("win")
    whitened = whitened.reshape(local_rows, 2, bands, FREQ_BINS // bands).transpose(2, 0, 1, 3)
    whitened = whitened.reshape(bands, local_rows, -1)
    windows = bands
    inverse_count = 1.0 / (windows * whitened.shape[2] // 2)
    col_set = spread_band(whitened, "cb")
    row_set = gather_by_permutes(spread_band(whitened, "cz"), "cx")
    operands = jnp.concatenate([col_set, swapped_parts(col_set, windows)], axis=0)
    product = jnp.einsum("ik,jk->ij", row_set, operands, precision=lax.Precision.HIGHEST)
    product = (product * inverse_count).astype(jnp.bfloat16)
    product = product.reshape(group_x * group_z, local_rows, operands.shape[0])
    mine = lax.all_to_all(product, ("cx", "cz"), split_axis=0, concat_axis=0, tiled=True)
    mine = mine.reshape(group_x * group_z, local_rows, 2, col_set.shape[0])
    cross_spectra = mine.transpose(2, 1, 0, 3).reshape(2, local_rows, -1)
    return cross_spectra[None]


def solution(mesh):
    chan_size = mesh.shape["chan"]
    outer = chan_size // ROW_GROUP
    grid = mesh.devices.reshape(outer // Z_GROUP, Z_GROUP, ROW_GROUP, mesh.shape["win"])
    sub_mesh = Mesh(grid, ("cx", "cz", "cb", "win"))
    return jax.shard_map(
        body,
        mesh=sub_mesh,
        in_specs=(P(CHAN, "win", None), P(), P(), P(CHAN)),
        out_specs=P("win", None, CHAN, None),
        check_vma=False,
    )
```

```python
import numpy as np
import jax
import jax.numpy as jnp
from jax import lax
from jax.sharding import Mesh, PartitionSpec as P

SAMPLES = 1024
FREQ_BINS = 128
FIRST_BIN = 8
SMOOTH_BINS = 4
MOST_REACH = 8
ROW_GROUP = 8
Z_GROUP = 4


FLOOR_POWER = 0.01

CHAN = ("cx", "cz", "cb")


def with_halo(x, width):
    devices, length = (lax.axis_size(CHAN), x.shape[0])
    up = [(i, (i + 1) % devices) for i in range(devices - 1)]
    down = [(j, i) for i, j in up]
    last = lax.slice_in_dim(x, length - width, length, axis=0)
    initial = lax.slice_in_dim(x, 0, width, axis=0)
    before = lax.ppermute(last, CHAN, up)
    after = lax.ppermute(initial, CHAN, down)
    return jnp.concatenate([before, x, after], axis=0)


def gather_blocks(block, axis):
    size = lax.axis_size(axis)
    copies = jnp.broadcast_to(block[None], (size,) + block.shape)
    every = lax.all_to_all(copies, axis, split_axis=0, concat_axis=0, tiled=True)
    return every.reshape(-1, block.shape[1])

def spread_band(per_band, axes):
    size = lax.axis_size(axes)
    bands, rows, width = per_band.shape
    copies = jnp.broadcast_to(per_band[None], (size, bands, rows, width)).reshape(size * bands, rows, width)
    every = lax.all_to_all(copies, axes + ("win",), split_axis=0, concat_axis=0, tiled=True)
    every = every.reshape(size, bands, rows, width).transpose(0, 2, 1, 3)
    return every.reshape(size * rows, bands * width)

def fourier_table():
    sample_ids = np.arange(SAMPLES)
    bin_ids = FIRST_BIN + np.arange(FREQ_BINS)
    angles = 2.0 * np.pi / SAMPLES * (sample_ids[:, None] * bin_ids[None, :] % SAMPLES)
    taper = 0.5 - 0.5 * np.cos(2.0 * np.pi / SAMPLES * (sample_ids + 0.5))
    weights = taper[:, None] / np.sqrt(SAMPLES)
    table = np.concatenate([weights * np.cos(angles), -weights * np.sin(angles)], axis=1)
    return jnp.asarray(table.astype(np.float32))


def smoothing_table():
    bin_ids = jnp.arange(FREQ_BINS, dtype=jnp.int32)
    nearby = (jnp.abs(bin_ids[:, None] - bin_ids[None, :]) <= SMOOTH_BINS).astype(jnp.float32)
    return nearby / jnp.sum(nearby, axis=0, keepdims=True)


def swapped_parts(flat, windows):
    parts = flat.reshape(flat.shape[:-1] + (windows, 2, -1))
    turned = jnp.stack([-parts[..., 1, :], parts[..., 0, :]], axis=-2)
    return turned.reshape(flat.shape)


def body(strain, seg_ids, dead, radius):
    local_rows = strain.shape[0]
    group_b = lax.axis_size("cb")
    group_x = lax.axis_size("cx")
    group_z = lax.axis_size("cz")
    device = (lax.axis_index("cx") * group_z + lax.axis_index("cz")) * group_b + lax.axis_index("cb")
    seg_padded = jnp.pad(seg_ids, (MOST_REACH, MOST_REACH), constant_values=-1)
    near_segs = lax.dynamic_slice_in_dim(
        seg_padded, device * local_rows, local_rows + 2 * MOST_REACH
    )
    segment_ids = jnp.arange(dead.shape[0], dtype=jnp.int32)
    dead_near = jnp.sum(
        jnp.where(near_segs[:, None] == segment_ids[None, :], dead[None, :], 0), axis=1
    )
    alive_near = jnp.where(near_segs >= 0, 1 - dead_near, 0)
    own_segs = near_segs[MOST_REACH : MOST_REACH + local_rows]
    alive_own = alive_near[MOST_REACH : MOST_REACH + local_rows].astype(jnp.float32)
    columns = jnp.arange(local_rows + 2 * MOST_REACH, dtype=jnp.int32)[None, :]
    offsets = columns - (jnp.arange(local_rows, dtype=jnp.int32)[:, None] + MOST_REACH)
    linked = (
        (jnp.abs(offsets) <= radius[:, None])
        & (near_segs[None, :] == own_segs[:, None])
        & (alive_near[None, :] > 0)
    )
    linked_f = linked.astype(jnp.float32)
    counts = jnp.maximum(jnp.sum(linked_f, axis=1), 1.0)
    fourier = fourier_table()
    extended = with_halo(strain, MOST_REACH)
    neighbor_sums = jnp.einsum(
        "cr,rwt->cwt", linked.astype(jnp.bfloat16), extended, preferred_element_type=jnp.float32
    )
    filtered = alive_own[:, None, None] * (
        strain.astype(jnp.float32) - neighbor_sums / counts[:, None, None]
    )
    spectra = jnp.einsum("cwt,tk->cwk", filtered, fourier, precision=lax.Precision.HIGHEST)
    power_bins = spectra[..., :FREQ_BINS] ** 2 + spectra[..., FREQ_BINS:] ** 2
    smoothed = jnp.einsum(
        "cwk,kj->cwj", power_bins, smoothing_table(), precision=lax.Precision.HIGHEST
    )
    inverse_amp = lax.rsqrt(jnp.maximum(smoothed, FLOOR_POWER))
    whitened = spectra * jnp.concatenate([inverse_amp, inverse_amp], axis=-1)
    bands = lax.axis_size("win")
    whitened = whitened.reshape(local_rows, 2, bands, FREQ_BINS // bands).transpose(2, 0, 1, 3)
    whitened = whitened.reshape(bands, local_rows, -1)
    windows = bands
    inverse_count = 1.0 / (windows * whitened.shape[2] // 2)
    col_set = spread_band(whitened, ("cz", "cb"))
    row_set = spread_band(whitened, ("cx",))
    operands = jnp.concatenate([col_set, swapped_parts(col_set, windows)], axis=0)
    product = jnp.einsum("ik,jk->ij", row_set, operands, precision=lax.Precision.HIGHEST)
    product = (product * inverse_count).astype(jnp.bfloat16)
    product = product.reshape(group_x, local_rows, operands.shape[0])
    mine = lax.all_to_all(product, "cx", split_axis=0, concat_axis=0, tiled=True)
    mine = mine.reshape(group_x, local_rows, 2, col_set.shape[0])
    cross_spectra = mine.transpose(2, 1, 0, 3).reshape(2, local_rows, -1)
    return cross_spectra[None]


def solution(mesh):
    chan_size = mesh.shape["chan"]
    outer = chan_size // ROW_GROUP
    grid = mesh.devices.reshape(outer // Z_GROUP, Z_GROUP, ROW_GROUP, mesh.shape["win"])
    sub_mesh = Mesh(grid, ("cx", "cz", "cb", "win"))
    return jax.shard_map(
        body,
        mesh=sub_mesh,
        in_specs=(P(CHAN, "win", None), P(), P(), P(CHAN)),
        out_specs=P("win", None, CHAN, None),
        check_vma=False,
    )
```

```python
import numpy as np
import jax
import jax.numpy as jnp
from jax import lax
from jax.sharding import Mesh, PartitionSpec as P

SAMPLES = 1024
FREQ_BINS = 128
FIRST_BIN = 8
SMOOTH_BINS = 4
MOST_REACH = 8
ROW_GROUP = 8
Z_GROUP = 4


FLOOR_POWER = 0.01

CHAN = ("cx", "cz", "cb")


def with_halo(x, width):
    devices, length = (lax.axis_size(CHAN), x.shape[0])
    up = [(i, (i + 1) % devices) for i in range(devices - 1)]
    down = [(j, i) for i, j in up]
    last = lax.slice_in_dim(x, length - width, length, axis=0)
    initial = lax.slice_in_dim(x, 0, width, axis=0)
    before = lax.ppermute(last, CHAN, up)
    after = lax.ppermute(initial, CHAN, down)
    return jnp.concatenate([before, x, after], axis=0)


def gather_blocks(block, axis):
    size = lax.axis_size(axis)
    copies = jnp.broadcast_to(block[None], (size,) + block.shape)
    every = lax.all_to_all(copies, axis, split_axis=0, concat_axis=0, tiled=True)
    return every.reshape(-1, block.shape[1])

def spread_band(per_band, axis):
    size = lax.axis_size(axis)
    bands, rows, width = per_band.shape
    copies = jnp.broadcast_to(per_band[None], (size, bands, rows, width)).reshape(size * bands, rows, width)
    every = lax.all_to_all(copies, (axis, "win"), split_axis=0, concat_axis=0, tiled=True)
    every = every.reshape(size, bands, rows, width).transpose(0, 2, 1, 3)
    return every.reshape(size * rows, bands * width)

def fourier_table():
    sample_ids = np.arange(SAMPLES)
    bin_ids = FIRST_BIN + np.arange(FREQ_BINS)
    angles = 2.0 * np.pi / SAMPLES * (sample_ids[:, None] * bin_ids[None, :] % SAMPLES)
    taper = 0.5 - 0.5 * np.cos(2.0 * np.pi / SAMPLES * (sample_ids + 0.5))
    weights = taper[:, None] / np.sqrt(SAMPLES)
    table = np.concatenate([weights * np.cos(angles), -weights * np.sin(angles)], axis=1)
    return jnp.asarray(table.astype(np.float32))


def smoothing_table():
    bin_ids = jnp.arange(FREQ_BINS, dtype=jnp.int32)
    nearby = (jnp.abs(bin_ids[:, None] - bin_ids[None, :]) <= SMOOTH_BINS).astype(jnp.float32)
    return nearby / jnp.sum(nearby, axis=0, keepdims=True)


def swapped_parts(flat, windows):
    parts = flat.reshape(flat.shape[:-1] + (windows, 2, -1))
    turned = jnp.stack([-parts[..., 1, :], parts[..., 0, :]], axis=-2)
    return turned.reshape(flat.shape)


def body(strain, seg_ids, dead, radius):
    local_rows = strain.shape[0]
    group_b = lax.axis_size("cb")
    group_x = lax.axis_size("cx")
    group_z = lax.axis_size("cz")
    device = (lax.axis_index("cx") * group_z + lax.axis_index("cz")) * group_b + lax.axis_index("cb")
    seg_padded = jnp.pad(seg_ids, (MOST_REACH, MOST_REACH), constant_values=-1)
    near_segs = lax.dynamic_slice_in_dim(
        seg_padded, device * local_rows, local_rows + 2 * MOST_REACH
    )
    segment_ids = jnp.arange(dead.shape[0], dtype=jnp.int32)
    dead_near = jnp.sum(
        jnp.where(near_segs[:, None] == segment_ids[None, :], dead[None, :], 0), axis=1
    )
    alive_near = jnp.where(near_segs >= 0, 1 - dead_near, 0)
    own_segs = near_segs[MOST_REACH : MOST_REACH + local_rows]
    alive_own = alive_near[MOST_REACH : MOST_REACH + local_rows].astype(jnp.float32)
    columns = jnp.arange(local_rows + 2 * MOST_REACH, dtype=jnp.int32)[None, :]
    offsets = columns - (jnp.arange(local_rows, dtype=jnp.int32)[:, None] + MOST_REACH)
    linked = (
        (jnp.abs(offsets) <= radius[:, None])
        & (near_segs[None, :] == own_segs[:, None])
        & (alive_near[None, :] > 0)
    )
    linked_f = linked.astype(jnp.float32)
    counts = jnp.maximum(jnp.sum(linked_f, axis=1), 1.0)
    fourier = fourier_table()
    extended = with_halo(strain, MOST_REACH)
    neighbor_sums = jnp.einsum(
        "cr,rwt->cwt", linked.astype(jnp.bfloat16), extended, preferred_element_type=jnp.float32
    )
    filtered = alive_own[:, None, None] * (
        strain.astype(jnp.float32) - neighbor_sums / counts[:, None, None]
    )
    spectra = jnp.einsum("cwt,tk->cwk", filtered, fourier, precision=lax.Precision.HIGHEST)
    power_bins = spectra[..., :FREQ_BINS] ** 2 + spectra[..., FREQ_BINS:] ** 2
    smoothed = jnp.einsum(
        "cwk,kj->cwj", power_bins, smoothing_table(), precision=lax.Precision.HIGHEST
    )
    inverse_amp = lax.rsqrt(jnp.maximum(smoothed, FLOOR_POWER))
    whitened = spectra * jnp.concatenate([inverse_amp, inverse_amp], axis=-1)
    bands = lax.axis_size("win")
    whitened = whitened.reshape(local_rows, 2, bands, FREQ_BINS // bands).transpose(2, 0, 1, 3)
    whitened = whitened.reshape(bands, local_rows, -1)
    windows = bands
    inverse_count = 1.0 / (windows * whitened.shape[2] // 2)
    col_set = spread_band(whitened, "cb")
    row_set = gather_blocks(spread_band(whitened, "cx"), "cz")
    operands = jnp.concatenate([col_set, swapped_parts(col_set, windows)], axis=0)
    product = jnp.einsum("ik,jk->ij", row_set, operands, precision=lax.Precision.HIGHEST)
    product = (product * inverse_count).astype(jnp.bfloat16)
    product = product.reshape(group_z * group_x, local_rows, operands.shape[0])
    mine = lax.all_to_all(product, ("cz", "cx"), split_axis=0, concat_axis=0, tiled=True)
    mine = mine.reshape(group_z, group_x, local_rows, 2, col_set.shape[0])
    cross_spectra = mine.transpose(3, 2, 1, 0, 4).reshape(2, local_rows, -1)
    return cross_spectra[None]


def solution(mesh):
    chan_size = mesh.shape["chan"]
    outer = chan_size // ROW_GROUP
    grid = mesh.devices.reshape(outer // Z_GROUP, Z_GROUP, ROW_GROUP, mesh.shape["win"])
    sub_mesh = Mesh(grid, ("cx", "cz", "cb", "win"))
    return jax.shard_map(
        body,
        mesh=sub_mesh,
        in_specs=(P(CHAN, "win", None), P(), P(), P(CHAN)),
        out_specs=P("win", None, CHAN, None),
        check_vma=False,
    )
```

```python
import numpy as np
import jax
import jax.numpy as jnp
from jax import lax
from jax.sharding import Mesh, PartitionSpec as P

SAMPLES = 1024
FREQ_BINS = 128
FIRST_BIN = 8
SMOOTH_BINS = 4
MOST_REACH = 8
ROW_GROUP = 8
Z_GROUP = 4
Y_NEAR = 4


FLOOR_POWER = 0.01

CHAN = ("cx", "cz", "cyh", "cyl")


def with_halo(x, width):
    devices, length = (lax.axis_size(CHAN), x.shape[0])
    up = [(i, (i + 1) % devices) for i in range(devices - 1)]
    down = [(j, i) for i, j in up]
    last = lax.slice_in_dim(x, length - width, length, axis=0)
    initial = lax.slice_in_dim(x, 0, width, axis=0)
    before = lax.ppermute(last, CHAN, up)
    after = lax.ppermute(initial, CHAN, down)
    return jnp.concatenate([before, x, after], axis=0)


def gather_blocks(block, axis):
    size = lax.axis_size(axis)
    copies = jnp.broadcast_to(block[None], (size,) + block.shape)
    every = lax.all_to_all(copies, axis, split_axis=0, concat_axis=0, tiled=True)
    return every.reshape(-1, block.shape[1])

def spread_band(per_band, axes):
    size = lax.axis_size(axes)
    bands, rows, width = per_band.shape
    copies = jnp.broadcast_to(per_band[None], (size, bands, rows, width)).reshape(size * bands, rows, width)
    every = lax.all_to_all(copies, axes + ("win",), split_axis=0, concat_axis=0, tiled=True)
    every = every.reshape(size, bands, rows, width).transpose(0, 2, 1, 3)
    return every.reshape(size * rows, bands * width)

def fourier_table():
    sample_ids = np.arange(SAMPLES)
    bin_ids = FIRST_BIN + np.arange(FREQ_BINS)
    angles = 2.0 * np.pi / SAMPLES * (sample_ids[:, None] * bin_ids[None, :] % SAMPLES)
    taper = 0.5 - 0.5 * np.cos(2.0 * np.pi / SAMPLES * (sample_ids + 0.5))
    weights = taper[:, None] / np.sqrt(SAMPLES)
    table = np.concatenate([weights * np.cos(angles), -weights * np.sin(angles)], axis=1)
    return jnp.asarray(table.astype(np.float32))


def smoothing_table():
    bin_ids = jnp.arange(FREQ_BINS, dtype=jnp.int32)
    nearby = (jnp.abs(bin_ids[:, None] - bin_ids[None, :]) <= SMOOTH_BINS).astype(jnp.float32)
    return nearby / jnp.sum(nearby, axis=0, keepdims=True)


def swapped_parts(flat, windows):
    parts = flat.reshape(flat.shape[:-1] + (windows, 2, -1))
    turned = jnp.stack([-parts[..., 1, :], parts[..., 0, :]], axis=-2)
    return turned.reshape(flat.shape)


def body(strain, seg_ids, dead, radius):
    local_rows = strain.shape[0]
    group_x = lax.axis_size("cx")
    group_l = lax.axis_size("cyl")
    device = lax.axis_index(CHAN)
    seg_padded = jnp.pad(seg_ids, (MOST_REACH, MOST_REACH), constant_values=-1)
    near_segs = lax.dynamic_slice_in_dim(
        seg_padded, device * local_rows, local_rows + 2 * MOST_REACH
    )
    segment_ids = jnp.arange(dead.shape[0], dtype=jnp.int32)
    dead_near = jnp.sum(
        jnp.where(near_segs[:, None] == segment_ids[None, :], dead[None, :], 0), axis=1
    )
    alive_near = jnp.where(near_segs >= 0, 1 - dead_near, 0)
    own_segs = near_segs[MOST_REACH : MOST_REACH + local_rows]
    alive_own = alive_near[MOST_REACH : MOST_REACH + local_rows].astype(jnp.float32)
    columns = jnp.arange(local_rows + 2 * MOST_REACH, dtype=jnp.int32)[None, :]
    offsets = columns - (jnp.arange(local_rows, dtype=jnp.int32)[:, None] + MOST_REACH)
    linked = (
        (jnp.abs(offsets) <= radius[:, None])
        & (near_segs[None, :] == own_segs[:, None])
        & (alive_near[None, :] > 0)
    )
    linked_f = linked.astype(jnp.float32)
    counts = jnp.maximum(jnp.sum(linked_f, axis=1), 1.0)
    fourier = fourier_table()
    extended = with_halo(strain, MOST_REACH)
    neighbor_sums = jnp.einsum(
        "cr,rwt->cwt", linked.astype(jnp.bfloat16), extended, preferred_element_type=jnp.float32
    )
    filtered = alive_own[:, None, None] * (
        strain.astype(jnp.float32) - neighbor_sums / counts[:, None, None]
    )
    spectra = jnp.einsum("cwt,tk->cwk", filtered, fourier, precision=lax.Precision.HIGHEST)
    power_bins = spectra[..., :FREQ_BINS] ** 2 + spectra[..., FREQ_BINS:] ** 2
    smoothed = jnp.einsum(
        "cwk,kj->cwj", power_bins, smoothing_table(), precision=lax.Precision.HIGHEST
    )
    inverse_amp = lax.rsqrt(jnp.maximum(smoothed, FLOOR_POWER))
    whitened = spectra * jnp.concatenate([inverse_amp, inverse_amp], axis=-1)
    bands = lax.axis_size("win")
    whitened = whitened.reshape(local_rows, 2, bands, FREQ_BINS // bands).transpose(2, 0, 1, 3)
    whitened = whitened.reshape(bands, local_rows, -1)
    windows = bands
    inverse_count = 1.0 / (windows * whitened.shape[2] // 2)
    col_set = spread_band(whitened, ("cz", "cyh"))
    row_set = gather_blocks(spread_band(whitened, ("cyl",)), "cx")
    operands = jnp.concatenate([col_set, swapped_parts(col_set, windows)], axis=0)
    product = jnp.einsum("ik,jk->ij", row_set, operands, precision=lax.Precision.HIGHEST)
    product = (product * inverse_count).astype(jnp.bfloat16)
    product = product.reshape(group_x * group_l, local_rows, operands.shape[0])
    mine = lax.all_to_all(product, ("cx", "cyl"), split_axis=0, concat_axis=0, tiled=True)
    mine = mine.reshape(group_x, group_l, local_rows, 2, -1, local_rows)
    mine = mine.transpose(3, 2, 0, 4, 1, 5)
    cross_spectra = mine.reshape(2, local_rows, -1)
    return cross_spectra[None]


def solution(mesh):
    chan_size = mesh.shape["chan"]
    outer = chan_size // ROW_GROUP
    grid = mesh.devices.reshape(outer // Z_GROUP, Z_GROUP, ROW_GROUP // Y_NEAR, Y_NEAR, mesh.shape["win"])
    sub_mesh = Mesh(grid, ("cx", "cz", "cyh", "cyl", "win"))
    return jax.shard_map(
        body,
        mesh=sub_mesh,
        in_specs=(P(CHAN, "win", None), P(), P(), P(CHAN)),
        out_specs=P("win", None, CHAN, None),
        check_vma=False,
    )
```

```python
import numpy as np
import jax
import jax.numpy as jnp
from jax import lax
from jax.sharding import Mesh, PartitionSpec as P

SAMPLES = 1024
FREQ_BINS = 128
FIRST_BIN = 8
SMOOTH_BINS = 4
MOST_REACH = 8
ROW_GROUP = 8
Z_GROUP = 4


FLOOR_POWER = 0.01

CHAN = ("cx", "cz", "cb")


def with_halo(x, width):
    devices, length = (lax.axis_size(CHAN), x.shape[0])
    up = [(i, (i + 1) % devices) for i in range(devices - 1)]
    down = [(j, i) for i, j in up]
    last = lax.slice_in_dim(x, length - width, length, axis=0)
    initial = lax.slice_in_dim(x, 0, width, axis=0)
    before = lax.ppermute(last, CHAN, up)
    after = lax.ppermute(initial, CHAN, down)
    return jnp.concatenate([before, x, after], axis=0)


def gather_blocks(block, axis):
    size = lax.axis_size(axis)
    copies = jnp.broadcast_to(block[None], (size,) + block.shape)
    every = lax.all_to_all(copies, axis, split_axis=0, concat_axis=0, tiled=True)
    return every.reshape(-1, block.shape[1])

def spread_band(per_band, axis):
    size = lax.axis_size(axis)
    bands, rows, width = per_band.shape
    copies = jnp.broadcast_to(per_band[None], (size, bands, rows, width)).reshape(size * bands, rows, width)
    every = lax.all_to_all(copies, (axis, "win"), split_axis=0, concat_axis=0, tiled=True)
    every = every.reshape(size, bands, rows, width).transpose(0, 2, 1, 3)
    return every.reshape(size * rows, bands * width)

def fourier_table():
    sample_ids = np.arange(SAMPLES)
    bin_ids = FIRST_BIN + np.arange(FREQ_BINS)
    angles = 2.0 * np.pi / SAMPLES * (sample_ids[:, None] * bin_ids[None, :] % SAMPLES)
    taper = 0.5 - 0.5 * np.cos(2.0 * np.pi / SAMPLES * (sample_ids + 0.5))
    weights = taper[:, None] / np.sqrt(SAMPLES)
    table = np.concatenate([weights * np.cos(angles), -weights * np.sin(angles)], axis=1)
    return jnp.asarray(table.astype(np.float32))


def smoothing_table():
    bin_ids = jnp.arange(FREQ_BINS, dtype=jnp.int32)
    nearby = (jnp.abs(bin_ids[:, None] - bin_ids[None, :]) <= SMOOTH_BINS).astype(jnp.float32)
    return nearby / jnp.sum(nearby, axis=0, keepdims=True)


def swapped_parts(flat, windows):
    parts = flat.reshape(flat.shape[:-1] + (windows, 2, -1))
    turned = jnp.stack([-parts[..., 1, :], parts[..., 0, :]], axis=-2)
    return turned.reshape(flat.shape)


def body(strain, seg_ids, dead, radius):
    local_rows = strain.shape[0]
    group_b = lax.axis_size("cb")
    group_x = lax.axis_size("cx")
    group_z = lax.axis_size("cz")
    device = (lax.axis_index("cx") * group_z + lax.axis_index("cz")) * group_b + lax.axis_index("cb")
    seg_padded = jnp.pad(seg_ids, (MOST_REACH, MOST_REACH), constant_values=-1)
    near_segs = lax.dynamic_slice_in_dim(
        seg_padded, device * local_rows, local_rows + 2 * MOST_REACH
    )
    dead_near = jnp.where(near_segs >= 0, dead[jnp.clip(near_segs, 0, dead.shape[0] - 1)], 0)
    alive_near = jnp.where(near_segs >= 0, 1 - dead_near, 0)
    own_segs = near_segs[MOST_REACH : MOST_REACH + local_rows]
    alive_own = alive_near[MOST_REACH : MOST_REACH + local_rows].astype(jnp.float32)
    columns = jnp.arange(local_rows + 2 * MOST_REACH, dtype=jnp.int32)[None, :]
    offsets = columns - (jnp.arange(local_rows, dtype=jnp.int32)[:, None] + MOST_REACH)
    linked = (
        (jnp.abs(offsets) <= radius[:, None])
        & (near_segs[None, :] == own_segs[:, None])
        & (alive_near[None, :] > 0)
    )
    linked_f = linked.astype(jnp.float32)
    counts = jnp.maximum(jnp.sum(linked_f, axis=1), 1.0)
    fourier = fourier_table()
    extended = with_halo(strain, MOST_REACH)
    neighbor_sums = jnp.einsum(
        "cr,rwt->cwt", linked.astype(jnp.bfloat16), extended, preferred_element_type=jnp.float32
    )
    filtered = alive_own[:, None, None] * (
        strain.astype(jnp.float32) - neighbor_sums / counts[:, None, None]
    )
    spectra = jnp.einsum("cwt,tk->cwk", filtered, fourier, precision=lax.Precision.HIGH)
    power_bins = spectra[..., :FREQ_BINS] ** 2 + spectra[..., FREQ_BINS:] ** 2
    smoothed = jnp.einsum(
        "cwk,kj->cwj", power_bins, smoothing_table(), precision=lax.Precision.HIGHEST
    )
    inverse_amp = lax.rsqrt(jnp.maximum(smoothed, FLOOR_POWER))
    whitened = spectra * jnp.concatenate([inverse_amp, inverse_amp], axis=-1)
    bands = lax.axis_size("win")
    whitened = whitened.reshape(local_rows, 2, bands, FREQ_BINS // bands).transpose(2, 0, 1, 3)
    whitened = whitened.reshape(bands, local_rows, -1)
    windows = bands
    inverse_count = 1.0 / (windows * whitened.shape[2] // 2)
    col_set = spread_band(whitened, "cb")
    row_set = gather_blocks(spread_band(whitened, "cz"), "cx")
    operands = jnp.concatenate([col_set, swapped_parts(col_set, windows)], axis=0)
    product = jnp.einsum("ik,jk->ij", row_set, operands, precision=lax.Precision.HIGH)
    product = (product * inverse_count).astype(jnp.bfloat16)
    product = product.reshape(group_x * group_z, local_rows, operands.shape[0])
    mine = lax.all_to_all(product, ("cx", "cz"), split_axis=0, concat_axis=0, tiled=True)
    mine = mine.reshape(group_x * group_z, local_rows, 2, col_set.shape[0])
    cross_spectra = mine.transpose(2, 1, 0, 3).reshape(2, local_rows, -1)
    return cross_spectra[None]


def solution(mesh):
    chan_size = mesh.shape["chan"]
    outer = chan_size // ROW_GROUP
    grid = mesh.devices.reshape(outer // Z_GROUP, Z_GROUP, ROW_GROUP, mesh.shape["win"])
    sub_mesh = Mesh(grid, ("cx", "cz", "cb", "win"))
    return jax.shard_map(
        body,
        mesh=sub_mesh,
        in_specs=(P(CHAN, "win", None), P(), P(), P(CHAN)),
        out_specs=P("win", None, CHAN, None),
        check_vma=False,
    )
```

```python
import numpy as np
import jax
import jax.numpy as jnp
from jax import lax
from jax.sharding import Mesh, PartitionSpec as P

SAMPLES = 1024
FREQ_BINS = 128
FIRST_BIN = 8
SMOOTH_BINS = 4
MOST_REACH = 8
ROW_GROUP = 8
Z_GROUP = 4


FLOOR_POWER = 0.01

CHAN = ("cx", "cz", "cb")


def with_halo(x, width):
    devices, length = (lax.axis_size(CHAN), x.shape[0])
    up = [(i, (i + 1) % devices) for i in range(devices - 1)]
    down = [(j, i) for i, j in up]
    last = lax.slice_in_dim(x, length - width, length, axis=0)
    initial = lax.slice_in_dim(x, 0, width, axis=0)
    before = lax.ppermute(last, CHAN, up)
    after = lax.ppermute(initial, CHAN, down)
    return jnp.concatenate([before, x, after], axis=0)


def gather_blocks(block, axis):
    size = lax.axis_size(axis)
    copies = jnp.broadcast_to(block[None], (size,) + block.shape)
    every = lax.all_to_all(copies, axis, split_axis=0, concat_axis=0, tiled=True)
    return every.reshape(-1, block.shape[1])

def spread_band(per_band, axis):
    size = lax.axis_size(axis)
    bands, rows, width = per_band.shape
    copies = jnp.broadcast_to(per_band[None], (size, bands, rows, width)).reshape(size * bands, rows, width)
    every = lax.all_to_all(copies, (axis, "win"), split_axis=0, concat_axis=0, tiled=True)
    every = every.reshape(size, bands, rows, width).transpose(0, 2, 1, 3)
    return every.reshape(size * rows, bands * width)

def fourier_table():
    sample_ids = np.arange(SAMPLES)
    bin_ids = FIRST_BIN + np.arange(FREQ_BINS)
    angles = 2.0 * np.pi / SAMPLES * (sample_ids[:, None] * bin_ids[None, :] % SAMPLES)
    taper = 0.5 - 0.5 * np.cos(2.0 * np.pi / SAMPLES * (sample_ids + 0.5))
    weights = taper[:, None] / np.sqrt(SAMPLES)
    table = np.concatenate([weights * np.cos(angles), -weights * np.sin(angles)], axis=1)
    return jnp.asarray(table.astype(np.float32))


def smoothing_table():
    bin_ids = jnp.arange(FREQ_BINS, dtype=jnp.int32)
    nearby = (jnp.abs(bin_ids[:, None] - bin_ids[None, :]) <= SMOOTH_BINS).astype(jnp.float32)
    return nearby / jnp.sum(nearby, axis=0, keepdims=True)


def swapped_parts(flat, windows):
    parts = flat.reshape(flat.shape[:-1] + (windows, 2, -1))
    turned = jnp.stack([-parts[..., 1, :], parts[..., 0, :]], axis=-2)
    return turned.reshape(flat.shape)


def body(strain, seg_ids, dead, radius):
    local_rows = strain.shape[0]
    group_b = lax.axis_size("cb")
    group_x = lax.axis_size("cx")
    group_z = lax.axis_size("cz")
    device = (lax.axis_index("cx") * group_z + lax.axis_index("cz")) * group_b + lax.axis_index("cb")
    seg_padded = jnp.pad(seg_ids, (MOST_REACH, MOST_REACH), constant_values=-1)
    near_segs = lax.dynamic_slice_in_dim(
        seg_padded, device * local_rows, local_rows + 2 * MOST_REACH
    )
    dead_near = jnp.where(near_segs >= 0, dead[jnp.clip(near_segs, 0, dead.shape[0] - 1)], 0)
    alive_near = jnp.where(near_segs >= 0, 1 - dead_near, 0)
    own_segs = near_segs[MOST_REACH : MOST_REACH + local_rows]
    alive_own = alive_near[MOST_REACH : MOST_REACH + local_rows].astype(jnp.float32)
    columns = jnp.arange(local_rows + 2 * MOST_REACH, dtype=jnp.int32)[None, :]
    offsets = columns - (jnp.arange(local_rows, dtype=jnp.int32)[:, None] + MOST_REACH)
    linked = (
        (jnp.abs(offsets) <= radius[:, None])
        & (near_segs[None, :] == own_segs[:, None])
        & (alive_near[None, :] > 0)
    )
    linked_f = linked.astype(jnp.float32)
    counts = jnp.maximum(jnp.sum(linked_f, axis=1), 1.0)
    fourier = fourier_table()
    link_weights = linked.astype(jnp.bfloat16)
    own_sums = jnp.einsum(
        "cr,rwt->cwt", link_weights[:, MOST_REACH:MOST_REACH + local_rows], strain,
        preferred_element_type=jnp.float32,
    )
    halo = with_halo(strain, MOST_REACH)
    ends = jnp.concatenate([halo[:MOST_REACH], halo[MOST_REACH + local_rows:]], axis=0)
    end_weights = jnp.concatenate(
        [link_weights[:, :MOST_REACH], link_weights[:, MOST_REACH + local_rows:]], axis=1
    )
    neighbor_sums = own_sums + jnp.einsum(
        "cr,rwt->cwt", end_weights, ends, preferred_element_type=jnp.float32
    )
    filtered = alive_own[:, None, None] * (
        strain.astype(jnp.float32) - neighbor_sums / counts[:, None, None]
    )
    spectra = jnp.einsum("cwt,tk->cwk", filtered, fourier, precision=lax.Precision.HIGH)
    power_bins = spectra[..., :FREQ_BINS] ** 2 + spectra[..., FREQ_BINS:] ** 2
    smoothed = jnp.einsum(
        "cwk,kj->cwj", power_bins, smoothing_table(), precision=lax.Precision.HIGHEST
    )
    inverse_amp = lax.rsqrt(jnp.maximum(smoothed, FLOOR_POWER))
    whitened = spectra * jnp.concatenate([inverse_amp, inverse_amp], axis=-1)
    bands = lax.axis_size("win")
    whitened = whitened.reshape(local_rows, 2, bands, FREQ_BINS // bands).transpose(2, 0, 1, 3)
    whitened = whitened.reshape(bands, local_rows, -1)
    windows = bands
    inverse_count = 1.0 / (windows * whitened.shape[2] // 2)
    col_set = spread_band(whitened, "cb")
    row_set = gather_blocks(spread_band(whitened, "cz"), "cx")
    operands = jnp.concatenate([col_set, swapped_parts(col_set, windows)], axis=0)
    product = jnp.einsum("ik,jk->ij", row_set, operands, precision=lax.Precision.HIGH)
    product = (product * inverse_count).astype(jnp.bfloat16)
    product = product.reshape(group_x * group_z, local_rows, operands.shape[0])
    mine = lax.all_to_all(product, ("cx", "cz"), split_axis=0, concat_axis=0, tiled=True)
    mine = mine.reshape(group_x * group_z, local_rows, 2, col_set.shape[0])
    cross_spectra = mine.transpose(2, 1, 0, 3).reshape(2, local_rows, -1)
    return cross_spectra[None]


def solution(mesh):
    chan_size = mesh.shape["chan"]
    outer = chan_size // ROW_GROUP
    grid = mesh.devices.reshape(outer // Z_GROUP, Z_GROUP, ROW_GROUP, mesh.shape["win"])
    sub_mesh = Mesh(grid, ("cx", "cz", "cb", "win"))
    return jax.shard_map(
        body,
        mesh=sub_mesh,
        in_specs=(P(CHAN, "win", None), P(), P(), P(CHAN)),
        out_specs=P("win", None, CHAN, None),
        check_vma=False,
    )
```

```python
import numpy as np
import jax
import jax.numpy as jnp
from jax import lax
from jax.sharding import Mesh, PartitionSpec as P

SAMPLES = 1024
FREQ_BINS = 128
FIRST_BIN = 8
SMOOTH_BINS = 4
MOST_REACH = 8
ROW_GROUP = 8
Z_GROUP = 4


FLOOR_POWER = 0.01

CHAN = ("cx", "cz", "cb")


def with_halo(x, width):
    devices, length = (lax.axis_size(CHAN), x.shape[0])
    up = [(i, (i + 1) % devices) for i in range(devices - 1)]
    down = [(j, i) for i, j in up]
    last = lax.slice_in_dim(x, length - width, length, axis=0)
    initial = lax.slice_in_dim(x, 0, width, axis=0)
    before = lax.ppermute(last, CHAN, up)
    after = lax.ppermute(initial, CHAN, down)
    return jnp.concatenate([before, x, after], axis=0)


def gather_blocks(block, axis):
    size = lax.axis_size(axis)
    copies = jnp.broadcast_to(block[None], (size,) + block.shape)
    every = lax.all_to_all(copies, axis, split_axis=0, concat_axis=0, tiled=True)
    return every.reshape(-1, block.shape[1])

def spread_band(per_band, axis):
    size = lax.axis_size(axis)
    bands, rows, width = per_band.shape
    copies = jnp.broadcast_to(per_band[None], (size, bands, rows, width)).reshape(size * bands, rows, width)
    every = lax.all_to_all(copies, (axis, "win"), split_axis=0, concat_axis=0, tiled=True)
    every = every.reshape(size, bands, rows, width).transpose(0, 2, 1, 3)
    return every.reshape(size * rows, bands * width)

def fourier_table():
    sample_ids = np.arange(SAMPLES)
    bin_ids = FIRST_BIN + np.arange(FREQ_BINS)
    angles = 2.0 * np.pi / SAMPLES * (sample_ids[:, None] * bin_ids[None, :] % SAMPLES)
    taper = 0.5 - 0.5 * np.cos(2.0 * np.pi / SAMPLES * (sample_ids + 0.5))
    weights = taper[:, None] / np.sqrt(SAMPLES)
    table = np.concatenate([weights * np.cos(angles), -weights * np.sin(angles)], axis=1)
    return jnp.asarray(table.astype(np.float32))


def smoothing_table():
    bin_ids = jnp.arange(FREQ_BINS, dtype=jnp.int32)
    nearby = (jnp.abs(bin_ids[:, None] - bin_ids[None, :]) <= SMOOTH_BINS).astype(jnp.float32)
    return nearby / jnp.sum(nearby, axis=0, keepdims=True)


def swapped_parts(flat, windows):
    parts = flat.reshape(flat.shape[:-1] + (windows, 2, -1))
    turned = jnp.stack([-parts[..., 1, :], parts[..., 0, :]], axis=-2)
    return turned.reshape(flat.shape)


def body(strain, seg_ids, dead, radius):
    local_rows = strain.shape[0]
    group_b = lax.axis_size("cb")
    group_x = lax.axis_size("cx")
    group_z = lax.axis_size("cz")
    device = (lax.axis_index("cx") * group_z + lax.axis_index("cz")) * group_b + lax.axis_index("cb")
    seg_padded = jnp.pad(seg_ids, (MOST_REACH, MOST_REACH), constant_values=-1)
    near_segs = lax.dynamic_slice_in_dim(
        seg_padded, device * local_rows, local_rows + 2 * MOST_REACH
    )
    dead_near = jnp.where(near_segs >= 0, dead[jnp.clip(near_segs, 0, dead.shape[0] - 1)], 0)
    alive_near = jnp.where(near_segs >= 0, 1 - dead_near, 0)
    own_segs = near_segs[MOST_REACH : MOST_REACH + local_rows]
    alive_own = alive_near[MOST_REACH : MOST_REACH + local_rows].astype(jnp.float32)
    columns = jnp.arange(local_rows + 2 * MOST_REACH, dtype=jnp.int32)[None, :]
    offsets = columns - (jnp.arange(local_rows, dtype=jnp.int32)[:, None] + MOST_REACH)
    linked = (
        (jnp.abs(offsets) <= radius[:, None])
        & (near_segs[None, :] == own_segs[:, None])
        & (alive_near[None, :] > 0)
    )
    linked_f = linked.astype(jnp.float32)
    counts = jnp.maximum(jnp.sum(linked_f, axis=1), 1.0)
    fourier = fourier_table()
    extended = with_halo(strain, MOST_REACH)
    neighbor_sums = jnp.einsum(
        "cr,rwt->cwt", linked.astype(jnp.bfloat16), extended, preferred_element_type=jnp.float32
    )
    filtered = alive_own[:, None, None] * (
        strain.astype(jnp.float32) - neighbor_sums / counts[:, None, None]
    )
    spectra = jnp.einsum("cwt,tk->cwk", filtered, fourier, precision=lax.Precision.HIGH)
    power_bins = spectra[..., :FREQ_BINS] ** 2 + spectra[..., FREQ_BINS:] ** 2
    smoothed = jnp.einsum(
        "cwk,kj->cwj", power_bins, smoothing_table(), precision=lax.Precision.HIGHEST
    )
    inverse_amp = lax.rsqrt(jnp.maximum(smoothed, FLOOR_POWER))
    whitened = spectra * jnp.concatenate([inverse_amp, inverse_amp], axis=-1)
    bands = lax.axis_size("win")
    whitened = whitened.reshape(local_rows, 2, bands, FREQ_BINS // bands).transpose(2, 0, 1, 3)
    whitened = whitened.reshape(bands, local_rows, -1)
    windows = bands
    inverse_count = 1.0 / (windows * whitened.shape[2] // 2)
    col_set = spread_band(whitened, "cb")
    row_set = gather_blocks(spread_band(whitened, "cz"), "cx")
    operands = jnp.concatenate([col_set, swapped_parts(col_set, windows)], axis=0)
    product = jnp.einsum("ik,jk->ij", row_set, operands, precision=lax.Precision.HIGH)
    product = (product * inverse_count).astype(jnp.bfloat16)
    product = product.reshape(group_x * group_z, local_rows, 2, col_set.shape[0]).transpose(0, 2, 1, 3)
    mine = lax.all_to_all(product, ("cx", "cz"), split_axis=0, concat_axis=0, tiled=True)
    cross_spectra = mine.transpose(1, 2, 0, 3).reshape(2, local_rows, -1)
    return cross_spectra[None]


def solution(mesh):
    chan_size = mesh.shape["chan"]
    outer = chan_size // ROW_GROUP
    grid = mesh.devices.reshape(outer // Z_GROUP, Z_GROUP, ROW_GROUP, mesh.shape["win"])
    sub_mesh = Mesh(grid, ("cx", "cz", "cb", "win"))
    return jax.shard_map(
        body,
        mesh=sub_mesh,
        in_specs=(P(CHAN, "win", None), P(), P(), P(CHAN)),
        out_specs=P("win", None, CHAN, None),
        check_vma=False,
    )
```

```python
import numpy as np
import jax
import jax.numpy as jnp
from jax import lax
from jax.sharding import Mesh, PartitionSpec as P

SAMPLES = 1024
FREQ_BINS = 128
FIRST_BIN = 8
SMOOTH_BINS = 4
MOST_REACH = 8
ROW_GROUP = 8
Z_GROUP = 4


FLOOR_POWER = 0.01

CHAN = ("cx", "cz", "cb")


def with_halo(x, width):
    devices, length = (lax.axis_size(CHAN), x.shape[0])
    up = [(i, (i + 1) % devices) for i in range(devices - 1)]
    down = [(j, i) for i, j in up]
    last = lax.slice_in_dim(x, length - width, length, axis=0)
    initial = lax.slice_in_dim(x, 0, width, axis=0)
    before = lax.ppermute(last, CHAN, up)
    after = lax.ppermute(initial, CHAN, down)
    return jnp.concatenate([before, x, after], axis=0)


def gather_blocks(block, axis):
    size = lax.axis_size(axis)
    copies = jnp.broadcast_to(block[None], (size,) + block.shape)
    every = lax.all_to_all(copies, axis, split_axis=0, concat_axis=0, tiled=True)
    return every.reshape(-1, block.shape[1])

def spread_band(per_band, axis, rows):
    size = lax.axis_size(axis)
    bands, flat = per_band.shape
    width = flat // rows
    copies = jnp.broadcast_to(per_band[None], (size, bands, flat)).reshape(size * bands, flat)
    every = lax.all_to_all(copies, (axis, "win"), split_axis=0, concat_axis=0, tiled=True)
    every = every.reshape(size, bands, rows, width).transpose(0, 2, 1, 3)
    return every.reshape(size * rows, bands * width)

def fourier_table():
    sample_ids = np.arange(SAMPLES)
    bin_ids = FIRST_BIN + np.arange(FREQ_BINS)
    angles = 2.0 * np.pi / SAMPLES * (sample_ids[:, None] * bin_ids[None, :] % SAMPLES)
    taper = 0.5 - 0.5 * np.cos(2.0 * np.pi / SAMPLES * (sample_ids + 0.5))
    weights = taper[:, None] / np.sqrt(SAMPLES)
    table = np.concatenate([weights * np.cos(angles), -weights * np.sin(angles)], axis=1)
    return jnp.asarray(table.astype(np.float32))


def smoothing_table():
    bin_ids = jnp.arange(FREQ_BINS, dtype=jnp.int32)
    nearby = (jnp.abs(bin_ids[:, None] - bin_ids[None, :]) <= SMOOTH_BINS).astype(jnp.float32)
    return nearby / jnp.sum(nearby, axis=0, keepdims=True)


def swapped_parts(flat, windows):
    parts = flat.reshape(flat.shape[:-1] + (windows, 2, -1))
    turned = jnp.stack([-parts[..., 1, :], parts[..., 0, :]], axis=-2)
    return turned.reshape(flat.shape)


def body(strain, seg_ids, dead, radius):
    local_rows = strain.shape[0]
    group_b = lax.axis_size("cb")
    group_x = lax.axis_size("cx")
    group_z = lax.axis_size("cz")
    device = (lax.axis_index("cx") * group_z + lax.axis_index("cz")) * group_b + lax.axis_index("cb")
    seg_padded = jnp.pad(seg_ids, (MOST_REACH, MOST_REACH), constant_values=-1)
    near_segs = lax.dynamic_slice_in_dim(
        seg_padded, device * local_rows, local_rows + 2 * MOST_REACH
    )
    dead_near = jnp.where(near_segs >= 0, dead[jnp.clip(near_segs, 0, dead.shape[0] - 1)], 0)
    alive_near = jnp.where(near_segs >= 0, 1 - dead_near, 0)
    own_segs = near_segs[MOST_REACH : MOST_REACH + local_rows]
    alive_own = alive_near[MOST_REACH : MOST_REACH + local_rows].astype(jnp.float32)
    columns = jnp.arange(local_rows + 2 * MOST_REACH, dtype=jnp.int32)[None, :]
    offsets = columns - (jnp.arange(local_rows, dtype=jnp.int32)[:, None] + MOST_REACH)
    linked = (
        (jnp.abs(offsets) <= radius[:, None])
        & (near_segs[None, :] == own_segs[:, None])
        & (alive_near[None, :] > 0)
    )
    linked_f = linked.astype(jnp.float32)
    counts = jnp.maximum(jnp.sum(linked_f, axis=1), 1.0)
    fourier = fourier_table()
    extended = with_halo(strain, MOST_REACH)
    neighbor_sums = jnp.einsum(
        "cr,rwt->cwt", linked.astype(jnp.bfloat16), extended, preferred_element_type=jnp.float32
    )
    filtered = alive_own[:, None, None] * (
        strain.astype(jnp.float32) - neighbor_sums / counts[:, None, None]
    )
    spectra = jnp.einsum("cwt,tk->cwk", filtered, fourier, precision=lax.Precision.HIGH)
    power_bins = spectra[..., :FREQ_BINS] ** 2 + spectra[..., FREQ_BINS:] ** 2
    smoothed = jnp.einsum(
        "cwk,kj->cwj", power_bins, smoothing_table(), precision=lax.Precision.HIGHEST
    )
    inverse_amp = lax.rsqrt(jnp.maximum(smoothed, FLOOR_POWER))
    whitened = spectra * jnp.concatenate([inverse_amp, inverse_amp], axis=-1)
    bands = lax.axis_size("win")
    whitened = whitened.reshape(local_rows, 2, bands, FREQ_BINS // bands).transpose(2, 0, 1, 3)
    whitened = whitened.reshape(bands, -1)
    windows = bands
    inverse_count = 1.0 / (windows * (FREQ_BINS // bands))
    col_set = spread_band(whitened, "cb", local_rows)
    row_set = gather_blocks(spread_band(whitened, "cz", local_rows), "cx")
    operands = jnp.concatenate([col_set, swapped_parts(col_set, windows)], axis=0)
    product = jnp.einsum("ik,jk->ij", row_set, operands, precision=lax.Precision.HIGH)
    product = (product * inverse_count).astype(jnp.bfloat16)
    product = product.reshape(group_x * group_z, local_rows, operands.shape[0])
    mine = lax.all_to_all(product, ("cx", "cz"), split_axis=0, concat_axis=0, tiled=True)
    mine = mine.reshape(group_x * group_z, local_rows, 2, col_set.shape[0])
    cross_spectra = mine.transpose(2, 1, 0, 3).reshape(2, local_rows, -1)
    return cross_spectra[None]


def solution(mesh):
    chan_size = mesh.shape["chan"]
    outer = chan_size // ROW_GROUP
    grid = mesh.devices.reshape(outer // Z_GROUP, Z_GROUP, ROW_GROUP, mesh.shape["win"])
    sub_mesh = Mesh(grid, ("cx", "cz", "cb", "win"))
    return jax.shard_map(
        body,
        mesh=sub_mesh,
        in_specs=(P(CHAN, "win", None), P(), P(), P(CHAN)),
        out_specs=P("win", None, CHAN, None),
        check_vma=False,
    )
```

```python
import numpy as np
import jax
import jax.numpy as jnp
from jax import lax
from jax.sharding import Mesh, PartitionSpec as P

SAMPLES = 1024
FREQ_BINS = 128
FIRST_BIN = 8
SMOOTH_BINS = 4
MOST_REACH = 8
ROW_GROUP = 8
Z_GROUP = 4


FLOOR_POWER = 0.01

CHAN = ("cx", "cz", "cb")


def with_halo(x, width):
    devices, length = (lax.axis_size(CHAN), x.shape[0])
    up = [(i, (i + 1) % devices) for i in range(devices - 1)]
    down = [(j, i) for i, j in up]
    last = lax.slice_in_dim(x, length - width, length, axis=0)
    initial = lax.slice_in_dim(x, 0, width, axis=0)
    before = lax.ppermute(last, CHAN, up)
    after = lax.ppermute(initial, CHAN, down)
    return jnp.concatenate([before, x, after], axis=0)


def gather_blocks(block, axis):
    size = lax.axis_size(axis)
    copies = jnp.broadcast_to(block[None], (size,) + block.shape)
    every = lax.all_to_all(copies, axis, split_axis=0, concat_axis=0, tiled=True)
    return every.reshape(-1, block.shape[1])

def spread_band(per_band, axis):
    size = lax.axis_size(axis)
    bands, rows, width = per_band.shape
    copies = jnp.broadcast_to(per_band[None], (size, bands, rows, width)).reshape(size * bands, rows, width)
    every = lax.all_to_all(copies, (axis, "win"), split_axis=0, concat_axis=0, tiled=True)
    every = every.reshape(size, bands, rows, width).transpose(0, 2, 1, 3)
    return every.reshape(size * rows, bands * width)

def fourier_table():
    sample_ids = np.arange(SAMPLES)
    bin_ids = FIRST_BIN + np.arange(FREQ_BINS)
    angles = 2.0 * np.pi / SAMPLES * (sample_ids[:, None] * bin_ids[None, :] % SAMPLES)
    taper = 0.5 - 0.5 * np.cos(2.0 * np.pi / SAMPLES * (sample_ids + 0.5))
    weights = taper[:, None] / np.sqrt(SAMPLES)
    table = np.concatenate([weights * np.cos(angles), -weights * np.sin(angles)], axis=1)
    return jnp.asarray(table.astype(np.float32))


def smoothing_table():
    bin_ids = jnp.arange(FREQ_BINS, dtype=jnp.int32)
    nearby = (jnp.abs(bin_ids[:, None] - bin_ids[None, :]) <= SMOOTH_BINS).astype(jnp.float32)
    return nearby / jnp.sum(nearby, axis=0, keepdims=True)


def swapped_parts(flat, windows):
    parts = flat.reshape(flat.shape[:-1] + (windows, 2, -1))
    turned = jnp.stack([-parts[..., 1, :], parts[..., 0, :]], axis=-2)
    return turned.reshape(flat.shape)


def body(strain, seg_ids, dead, radius):
    local_rows = strain.shape[0]
    group_b = lax.axis_size("cb")
    group_x = lax.axis_size("cx")
    group_z = lax.axis_size("cz")
    device = (lax.axis_index("cx") * group_z + lax.axis_index("cz")) * group_b + lax.axis_index("cb")
    seg_padded = jnp.pad(seg_ids, (MOST_REACH, MOST_REACH), constant_values=-1)
    near_segs = lax.dynamic_slice_in_dim(
        seg_padded, device * local_rows, local_rows + 2 * MOST_REACH
    )
    dead_near = jnp.where(near_segs >= 0, dead[jnp.clip(near_segs, 0, dead.shape[0] - 1)], 0)
    alive_near = jnp.where(near_segs >= 0, 1 - dead_near, 0)
    own_segs = near_segs[MOST_REACH : MOST_REACH + local_rows]
    alive_own = alive_near[MOST_REACH : MOST_REACH + local_rows].astype(jnp.float32)
    columns = jnp.arange(local_rows + 2 * MOST_REACH, dtype=jnp.int32)[None, :]
    offsets = columns - (jnp.arange(local_rows, dtype=jnp.int32)[:, None] + MOST_REACH)
    linked = (
        (jnp.abs(offsets) <= radius[:, None])
        & (near_segs[None, :] == own_segs[:, None])
        & (alive_near[None, :] > 0)
    )
    linked_f = linked.astype(jnp.float32)
    counts = jnp.maximum(jnp.sum(linked_f, axis=1), 1.0)
    fourier = fourier_table()
    extended = with_halo(strain, MOST_REACH)
    neighbor_sums = jnp.einsum(
        "cr,rwt->cwt", linked.astype(jnp.bfloat16), extended, preferred_element_type=jnp.float32
    )
    filtered = alive_own[:, None, None] * (
        strain.astype(jnp.float32) - neighbor_sums / counts[:, None, None]
    )
    spectra = jnp.einsum("cwt,tk->cwk", filtered, fourier, precision=lax.Precision.HIGH)
    power_bins = spectra[..., :FREQ_BINS] ** 2 + spectra[..., FREQ_BINS:] ** 2
    smoothed = jnp.einsum(
        "cwk,kj->cwj", power_bins, smoothing_table(), precision=lax.Precision.HIGHEST
    )
    inverse_amp = lax.rsqrt(jnp.maximum(smoothed, FLOOR_POWER))
    whitened = spectra * jnp.concatenate([inverse_amp, inverse_amp], axis=-1)
    bands = lax.axis_size("win")
    whitened = whitened.reshape(local_rows, 2, bands, FREQ_BINS // bands).transpose(2, 0, 1, 3)
    whitened = whitened.reshape(bands, local_rows, -1)
    windows = bands
    inverse_count = 1.0 / (windows * whitened.shape[2] // 2)
    col_set = spread_band(whitened, "cb")
    col_set, whitened = lax.optimization_barrier((col_set, whitened))
    row_set = gather_blocks(spread_band(whitened, "cz"), "cx")
    operands = jnp.concatenate([col_set, swapped_parts(col_set, windows)], axis=0)
    product = jnp.einsum("ik,jk->ij", row_set, operands, precision=lax.Precision.HIGH)
    product = (product * inverse_count).astype(jnp.bfloat16)
    product = product.reshape(group_x * group_z, local_rows, operands.shape[0])
    mine = lax.all_to_all(product, ("cx", "cz"), split_axis=0, concat_axis=0, tiled=True)
    mine = mine.reshape(group_x * group_z, local_rows, 2, col_set.shape[0])
    cross_spectra = mine.transpose(2, 1, 0, 3).reshape(2, local_rows, -1)
    return cross_spectra[None]


def solution(mesh):
    chan_size = mesh.shape["chan"]
    outer = chan_size // ROW_GROUP
    grid = mesh.devices.reshape(outer // Z_GROUP, Z_GROUP, ROW_GROUP, mesh.shape["win"])
    sub_mesh = Mesh(grid, ("cx", "cz", "cb", "win"))
    return jax.shard_map(
        body,
        mesh=sub_mesh,
        in_specs=(P(CHAN, "win", None), P(), P(), P(CHAN)),
        out_specs=P("win", None, CHAN, None),
        check_vma=False,
    )
```

```python
import numpy as np
import jax
import jax.numpy as jnp
from jax import lax
from jax.sharding import Mesh, PartitionSpec as P

SAMPLES = 1024
FREQ_BINS = 128
FIRST_BIN = 8
SMOOTH_BINS = 4
MOST_REACH = 8
ROW_GROUP = 8
Z_GROUP = 4


FLOOR_POWER = 0.01

CHAN = ("cx", "cz", "cb")


def with_halo(x, width):
    devices, length = (lax.axis_size(CHAN), x.shape[0])
    up = [(i, (i + 1) % devices) for i in range(devices - 1)]
    down = [(j, i) for i, j in up]
    last = lax.slice_in_dim(x, length - width, length, axis=0)
    initial = lax.slice_in_dim(x, 0, width, axis=0)
    before = lax.ppermute(last, CHAN, up)
    after = lax.ppermute(initial, CHAN, down)
    return jnp.concatenate([before, x, after], axis=0)


def gather_blocks(block, axis):
    size = lax.axis_size(axis)
    copies = jnp.broadcast_to(block[None], (size,) + block.shape)
    every = lax.all_to_all(copies, axis, split_axis=0, concat_axis=0, tiled=True)
    return every.reshape(-1, block.shape[1])

def spread_band(per_band, axis):
    size = lax.axis_size(axis)
    bands, rows, width = per_band.shape
    copies = jnp.broadcast_to(per_band[None], (size, bands, rows, width)).reshape(size * bands, rows, width)
    every = lax.all_to_all(copies, (axis, "win"), split_axis=0, concat_axis=0, tiled=True)
    every = every.reshape(size, bands, rows, width).transpose(0, 2, 1, 3)
    return every.reshape(size * rows, bands * width)

def gather_by_permutes(block, axis):
    size = lax.axis_size(axis)
    me = lax.axis_index(axis)
    pieces = [block]
    for shift in range(1, size):
        pairs = [(src, (src - shift) % size) for src in range(size)]
        pieces.append(lax.ppermute(block, axis, pairs))
    rel = jnp.concatenate(pieces + pieces, axis=0)
    rows = block.shape[0]
    start = ((size - me) % size) * rows
    return lax.dynamic_slice_in_dim(rel, start, size * rows, axis=0)

def fourier_table():
    sample_ids = np.arange(SAMPLES)
    bin_ids = FIRST_BIN + np.arange(FREQ_BINS)
    angles = 2.0 * np.pi / SAMPLES * (sample_ids[:, None] * bin_ids[None, :] % SAMPLES)
    taper = 0.5 - 0.5 * np.cos(2.0 * np.pi / SAMPLES * (sample_ids + 0.5))
    weights = taper[:, None] / np.sqrt(SAMPLES)
    table = np.concatenate([weights * np.cos(angles), -weights * np.sin(angles)], axis=1)
    return jnp.asarray(table.astype(np.float32))


def smoothing_table():
    bin_ids = jnp.arange(FREQ_BINS, dtype=jnp.int32)
    nearby = (jnp.abs(bin_ids[:, None] - bin_ids[None, :]) <= SMOOTH_BINS).astype(jnp.float32)
    return nearby / jnp.sum(nearby, axis=0, keepdims=True)


def swapped_parts(flat, windows):
    parts = flat.reshape(flat.shape[:-1] + (windows, 2, -1))
    turned = jnp.stack([-parts[..., 1, :], parts[..., 0, :]], axis=-2)
    return turned.reshape(flat.shape)


def body(strain, seg_ids, dead, radius):
    local_rows = strain.shape[0]
    group_b = lax.axis_size("cb")
    group_x = lax.axis_size("cx")
    group_z = lax.axis_size("cz")
    device = (lax.axis_index("cx") * group_z + lax.axis_index("cz")) * group_b + lax.axis_index("cb")
    seg_padded = jnp.pad(seg_ids, (MOST_REACH, MOST_REACH), constant_values=-1)
    near_segs = lax.dynamic_slice_in_dim(
        seg_padded, device * local_rows, local_rows + 2 * MOST_REACH
    )
    dead_near = jnp.where(near_segs >= 0, dead[jnp.clip(near_segs, 0, dead.shape[0] - 1)], 0)
    alive_near = jnp.where(near_segs >= 0, 1 - dead_near, 0)
    own_segs = near_segs[MOST_REACH : MOST_REACH + local_rows]
    alive_own = alive_near[MOST_REACH : MOST_REACH + local_rows].astype(jnp.float32)
    columns = jnp.arange(local_rows + 2 * MOST_REACH, dtype=jnp.int32)[None, :]
    offsets = columns - (jnp.arange(local_rows, dtype=jnp.int32)[:, None] + MOST_REACH)
    linked = (
        (jnp.abs(offsets) <= radius[:, None])
        & (near_segs[None, :] == own_segs[:, None])
        & (alive_near[None, :] > 0)
    )
    linked_f = linked.astype(jnp.float32)
    counts = jnp.maximum(jnp.sum(linked_f, axis=1), 1.0)
    fourier = fourier_table()
    extended = with_halo(strain, MOST_REACH)
    neighbor_sums = jnp.einsum(
        "cr,rwt->cwt", linked.astype(jnp.bfloat16), extended, preferred_element_type=jnp.float32
    )
    filtered = alive_own[:, None, None] * (
        strain.astype(jnp.float32) - neighbor_sums / counts[:, None, None]
    )
    spectra = jnp.einsum("cwt,tk->cwk", filtered, fourier, precision=lax.Precision.HIGH)
    power_bins = spectra[..., :FREQ_BINS] ** 2 + spectra[..., FREQ_BINS:] ** 2
    smoothed = jnp.einsum(
        "cwk,kj->cwj", power_bins, smoothing_table(), precision=lax.Precision.HIGHEST
    )
    inverse_amp = lax.rsqrt(jnp.maximum(smoothed, FLOOR_POWER))
    whitened = spectra * jnp.concatenate([inverse_amp, inverse_amp], axis=-1)
    bands = lax.axis_size("win")
    whitened = whitened.reshape(local_rows, 2, bands, FREQ_BINS // bands).transpose(2, 0, 1, 3)
    whitened = whitened.reshape(bands, local_rows, -1)
    windows = bands
    inverse_count = 1.0 / (windows * whitened.shape[2] // 2)
    col_set = spread_band(whitened, "cb")
    row_set = gather_by_permutes(spread_band(whitened, "cz"), "cx")
    operands = jnp.concatenate([col_set, swapped_parts(col_set, windows)], axis=0)
    product = jnp.einsum("ik,jk->ij", row_set, operands, precision=lax.Precision.HIGH)
    product = (product * inverse_count).astype(jnp.bfloat16)
    product = product.reshape(group_x * group_z, local_rows, operands.shape[0])
    mine = lax.all_to_all(product, ("cx", "cz"), split_axis=0, concat_axis=0, tiled=True)
    mine = mine.reshape(group_x * group_z, local_rows, 2, col_set.shape[0])
    cross_spectra = mine.transpose(2, 1, 0, 3).reshape(2, local_rows, -1)
    return cross_spectra[None]


def solution(mesh):
    chan_size = mesh.shape["chan"]
    outer = chan_size // ROW_GROUP
    grid = mesh.devices.reshape(outer // Z_GROUP, Z_GROUP, ROW_GROUP, mesh.shape["win"])
    sub_mesh = Mesh(grid, ("cx", "cz", "cb", "win"))
    return jax.shard_map(
        body,
        mesh=sub_mesh,
        in_specs=(P(CHAN, "win", None), P(), P(), P(CHAN)),
        out_specs=P("win", None, CHAN, None),
        check_vma=False,
    )
```
